512 devices in a mesh: section: 8 (over x, z_lo), dp: 64 (over y, z_hi, core).
Axes of the slice: x: 4, y: 8, z: 8 (z_hi: 4, z_lo: 2; z = z_hi * 2 + z_lo), core: 2. Of those that a mesh axis runs over, the one named last changes fastest.
Arguments:
- saved_input: bfloat16 [8, 256, 4096], P('section', 'dp'), may hold values from -6 to 6
- grad_sent: bfloat16 [8, 256, 4096], P('section', 'dp'), may hold values from -6 to 6
- kept_blocks: int32 [8, 1664], P('section', 'dp'), may hold values from 0 to 63, as said below
- gate_blocks: bfloat16 [8, 1664, 128, 128], P('section', 'dp'), may hold values from -0.15625 to 0.15625
- up_blocks: bfloat16 [8, 1664, 128, 128], P('section', 'dp'), may hold values from -0.15625 to 0.15625
- down_blocks: bfloat16 [8, 1664, 128, 128], P('section', 'dp'), may hold values from -0.078125 to 0.078125
Outputs:
- grad_input: bfloat16 [8, 256, 4096], P('section', 'dp')
- grad_gate: bfloat16 [8, 1664, 128, 128], P('section', 'dp')
- grad_up: bfloat16 [8, 1664, 128, 128], P('section', 'dp')
- grad_down: bfloat16 [8, 1664, 128, 128], P('section', 'dp')
The draws below stay inside these ranges and needn't reach their ends.
Inputs may be any that keep to these rules, and one draw needn't show every extreme that they name: `kept_blocks`: each device's 26 ids are different and increasing; an id is the band along the model width times 2 plus the block among that device's hidden units; bands keep unequal shares of their blocks.
All inputs are finite; a program needn't handle non-finite values.
Results may differ from the reference program's by a relative error of at most 0.019.
Values may be sent and summed in bfloat16 or wider, within the bound.
No kernel may reach another device: no remote copies, remote signals or barrier semaphores. Data moves between devices by JAX's collectives and lax.ppermute only.
A program may use at most 64 MiB of HBM per device.

```python
import jax
import jax.numpy as jnp
from jax import lax

D = 4096
BLOCK = 128
KEPT = 26
ROWS = 256
LAYERS = 8
BANDS = 32
CB_DEV = 2
N_DP = 64


def draw_kept_blocks(key, part):
    key_band = jax.random.fold_in(key, 11)
    key_cell = jax.random.fold_in(key, 23)
    total = BANDS * CB_DEV
    band_weight = jax.random.randint(key_band, (LAYERS, N_DP, BANDS, 1), 0, 4)
    cell_score = jax.random.randint(key_cell, (LAYERS, N_DP, BANDS, CB_DEV), 0, 64)
    score = (cell_score + 32 * band_weight).reshape(LAYERS, N_DP, total)
    distinct = score * total + jnp.arange(total, dtype=jnp.int32)
    picked = lax.top_k(distinct, KEPT)[1].astype(jnp.int32)
    picked = jnp.sort(picked, axis=-1)
    return picked.reshape(LAYERS, N_DP * KEPT)


def block_levels(key, dims, cuts, low, top_value):
    factor_of, own = 1.0, jax.random.fold_in(key, 6)
    for dim, parts in cuts:
        steps = jnp.exp(jax.random.uniform(jax.random.fold_in(own, dim), (parts,), jnp.float32, low / len(cuts), top_value / len(cuts)))
        factor_of = factor_of * jnp.repeat(steps, dims[dim] // parts).reshape([-1 if axis == dim else 1 for axis in range(len(dims))])
    return factor_of


def noise(key, shape, spread, limit, pieces=(), held_as=jnp.bfloat16):
    drawn = spread * jax.random.normal(key, shape, jnp.float32)
    if pieces:
        drawn = drawn * block_levels(key, shape, pieces, -0.22, 0.18)
    return jnp.clip(drawn, -limit, limit).astype(held_as)


def setup_inputs(seed: int = 0) -> dict:
    key_of = jax.random.split(jax.random.key(seed), 7)
    saved_input = noise(key_of[0], (LAYERS, ROWS, D), 1.0, 6.0, ((0, 8), (1, 64)))
    grad_sent = noise(key_of[1], (LAYERS, ROWS, D), 1.0, 6.0, ((0, 8), (1, 64)))
    kept_blocks = draw_kept_blocks(jax.random.fold_in(key_of[6], 71), 0)
    gate_blocks = noise(key_of[3], (LAYERS, N_DP * KEPT, BLOCK, BLOCK), (BLOCK * KEPT // CB_DEV) ** -0.5, 0.15625, ((0, 8), (1, 64)))
    up_blocks = noise(key_of[4], (LAYERS, N_DP * KEPT, BLOCK, BLOCK), (BLOCK * KEPT // CB_DEV) ** -0.5, 0.15625, ((0, 8), (1, 64)))
    down_blocks = noise(key_of[5], (LAYERS, N_DP * KEPT, BLOCK, BLOCK), (BLOCK * N_DP * KEPT // BANDS) ** -0.5, 0.078125, ((0, 8), (1, 64)))
    return dict(saved_input=saved_input, grad_sent=grad_sent, kept_blocks=kept_blocks, gate_blocks=gate_blocks, up_blocks=up_blocks, down_blocks=down_blocks)


def one_group(inputs, upstream, ids, wg, wu, wd):
    band = (ids // CB_DEV).astype(jnp.int32)
    col = (ids % CB_DEV).astype(jnp.int32)
    col_onehot = (col[:, None] == jnp.arange(CB_DEV, dtype=jnp.int32)[None, :]).astype(jnp.float32)
    band_onehot = (band[:, None] == jnp.arange(BANDS, dtype=jnp.int32)[None, :]).astype(jnp.float32)
    rows = inputs.shape[0]
    input_sel = jnp.take(inputs.reshape(rows, BANDS, BLOCK), band, axis=1).astype(jnp.float32)
    grad_sel = jnp.take(upstream.reshape(rows, BANDS, BLOCK), band, axis=1).astype(jnp.float32)
    wg32 = wg.astype(jnp.float32)
    wu32 = wu.astype(jnp.float32)
    wd32 = wd.astype(jnp.float32)

    def to_columns(partial_value):
        return jnp.einsum("tkc,kn->tnc", partial_value, col_onehot).reshape(rows, CB_DEV * BLOCK)

    def pick_cols(values):
        return jnp.take(values.reshape(rows, CB_DEV, BLOCK), col, axis=1).astype(jnp.float32)

    gate = to_columns(jnp.einsum("tkb,kbc->tkc", input_sel, wg32))
    up = to_columns(jnp.einsum("tkb,kbc->tkc", input_sel, wu32))
    sig = jax.nn.sigmoid(gate)
    act = gate * sig
    hidden = (act * up).astype(jnp.bfloat16)
    dhid = to_columns(jnp.einsum("tkb,kcb->tkc", grad_sel, wd32))
    dup = (dhid * act).astype(jnp.bfloat16)
    dgate = (dhid * up * sig * (1.0 + gate * (1.0 - sig))).astype(jnp.bfloat16)
    tile_d = jnp.einsum("tkc,tkb->kcb", pick_cols(hidden), grad_sel).astype(jnp.bfloat16)
    tile_g = jnp.einsum("tkb,tkc->kbc", input_sel, pick_cols(dgate)).astype(jnp.bfloat16)
    tile_u = jnp.einsum("tkb,tkc->kbc", input_sel, pick_cols(dup)).astype(jnp.bfloat16)
    slots = jnp.einsum("tkc,kbc->tkb", pick_cols(dgate), wg32)
    slots = slots + jnp.einsum("tkc,kbc->tkb", pick_cols(dup), wu32)
    part = jnp.einsum("tkb,kr->trb", slots, band_onehot).reshape(rows, BANDS * BLOCK)
    return part, tile_g, tile_u, tile_d


def reference(saved_input, grad_sent, kept_blocks, gate_blocks, up_blocks, down_blocks):
    outs_dx, outs_g, outs_u, outs_d = [], [], [], []
    for layer in range(LAYERS):
        inputs = saved_input[layer]
        upstream = grad_sent[(layer + 1) % LAYERS]
        ids = kept_blocks[layer].reshape(N_DP, KEPT)
        wg = gate_blocks[layer].reshape(N_DP, KEPT, BLOCK, BLOCK)
        wu = up_blocks[layer].reshape(N_DP, KEPT, BLOCK, BLOCK)
        wd = down_blocks[layer].reshape(N_DP, KEPT, BLOCK, BLOCK)

        def step(carry, item):
            gid, tg, tu, td = item
            part, tile_g, tile_u, tile_d = one_group(inputs, upstream, gid, tg, tu, td)
            return carry + part, (tile_g, tile_u, tile_d)

        start = jnp.zeros((ROWS, D), jnp.float32)
        total, (tiles_g, tiles_u, tiles_d) = lax.scan(step, start, (ids, wg, wu, wd))
        outs_dx.append(total.astype(jnp.bfloat16))
        outs_g.append(tiles_g.reshape(N_DP * KEPT, BLOCK, BLOCK))
        outs_u.append(tiles_u.reshape(N_DP * KEPT, BLOCK, BLOCK))
        outs_d.append(tiles_d.reshape(N_DP * KEPT, BLOCK, BLOCK))
    return (jnp.stack(outs_dx), jnp.stack(outs_g), jnp.stack(outs_u), jnp.stack(outs_d))
```

```python
import jax
import jax.numpy as jnp
from jax import lax
from jax.sharding import Mesh, PartitionSpec as P

FF = 16384
ROW_AXES = ("y", "zh", "core")


def passed_along(block, axis, distance):
    devices = range(lax.axis_size(axis))
    route = [((i - distance) % len(devices), i) for i in devices]
    return lax.ppermute(block, axis, route)


def gather_rows(block):
    for axis in ("zh", "y", "core"):
        block = lax.all_gather(block, axis, axis=1, tiled=True)
    return block


def scatter_rows(block):
    for axis in ("core", "y", "zh"):
        block = lax.psum_scatter(block, axis, scatter_dimension=0, tiled=True)
    return block


def per_device(saved_input, grad_sent, kept_blocks, gate_blocks, up_blocks, down_blocks):
    width = saved_input.shape[2]
    block = gate_blocks.shape[2]
    bands = width // block
    n_dp = 1
    for axis in ROW_AXES:
        n_dp *= lax.axis_size(axis)
    columns = FF // n_dp // block
    ids = kept_blocks[0]
    band_ids = ids // columns
    col_ids = ids % columns
    w_gate = gate_blocks[0]
    w_up = up_blocks[0]
    w_down = down_blocks[0]
    col_onehot = (col_ids[:, None] == jnp.arange(columns, dtype=jnp.int32)[None, :]).astype(
        jnp.float32
    )
    band_onehot = (band_ids[:, None] == jnp.arange(bands, dtype=jnp.int32)[None, :]).astype(
        jnp.float32
    )

    def to_columns(partial_value):
        spread = jnp.einsum("tkc,kn->tnc", partial_value, col_onehot)
        return spread.reshape(partial_value.shape[0], columns * block)

    def pick_cols(values):
        return jnp.take(values.reshape(values.shape[0], columns, block), col_ids, axis=1)

    def pick_bands(values):
        return jnp.take(values.reshape(values.shape[0], bands, block), band_ids, axis=1)

    incoming = passed_along(grad_sent, "section", -1)
    both = gather_rows(jnp.concatenate([saved_input, incoming], axis=0))
    inputs = both[0]
    upstream = both[1]
    chosen = pick_bands(inputs)
    gate = to_columns(
        jnp.einsum("tkb,kbc->tkc", chosen, w_gate, preferred_element_type=jnp.float32)
    )
    up = to_columns(jnp.einsum("tkb,kbc->tkc", chosen, w_up, preferred_element_type=jnp.float32))
    sig = jax.nn.sigmoid(gate)
    act = gate * sig
    hidden = (act * up).astype(jnp.bfloat16)
    grad_sel = pick_bands(upstream)
    dhid = to_columns(
        jnp.einsum("tkb,kcb->tkc", grad_sel, w_down, preferred_element_type=jnp.float32)
    )
    grad_up_act = (dhid * act).astype(jnp.bfloat16)
    grad_gate_act = (dhid * up * sig * (1.0 + gate * (1.0 - sig))).astype(jnp.bfloat16)
    input_sel = chosen
    tiles_down = jnp.einsum(
        "tkc,tkb->kcb", pick_cols(hidden), grad_sel, preferred_element_type=jnp.float32
    )
    tiles_gate = jnp.einsum(
        "tkb,tkc->kbc", input_sel, pick_cols(grad_gate_act), preferred_element_type=jnp.float32
    )
    tiles_up = jnp.einsum(
        "tkb,tkc->kbc", input_sel, pick_cols(grad_up_act), preferred_element_type=jnp.float32
    )
    slots = jnp.einsum(
        "tkc,kbc->tkb", pick_cols(grad_gate_act), w_gate, preferred_element_type=jnp.float32
    )
    slots = slots + jnp.einsum(
        "tkc,kbc->tkb", pick_cols(grad_up_act), w_up, preferred_element_type=jnp.float32
    )
    spread = jnp.einsum("tkb,kr->trb", slots, band_onehot)
    whole_term = spread.reshape(grad_gate_act.shape[0], bands * block)
    summed = scatter_rows(whole_term)
    grad_input = summed.astype(jnp.bfloat16)[None]
    return (
        grad_input,
        tiles_gate.astype(jnp.bfloat16)[None],
        tiles_up.astype(jnp.bfloat16)[None],
        tiles_down.astype(jnp.bfloat16)[None],
    )


def solution(mesh):
    n_dp = mesh.shape["dp"]
    split = Mesh(
        mesh.devices.reshape(mesh.shape["section"], n_dp // 8, 4, 2),
        ("section",) + ROW_AXES,
    )
    rows = P("section", ROW_AXES, None)
    blocks = P("section", ROW_AXES, None, None)
    return jax.shard_map(
        per_device,
        mesh=split,
        in_specs=(rows, rows, P("section", ROW_AXES), blocks, blocks, blocks),
        out_specs=(rows, blocks, blocks, blocks),
        check_vma=False,
    )
```

```python
import jax
import jax.numpy as jnp
from jax import lax
from jax.sharding import Mesh, PartitionSpec as P

FF = 16384
ROW_AXES = ("y", "zh", "core")


def passed_along(block, axis, distance):
    devices = range(lax.axis_size(axis))
    route = [((i - distance) % len(devices), i) for i in devices]
    return lax.ppermute(block, axis, route)


def shifted(block, axis, shift):
    n = lax.axis_size(axis)
    return lax.ppermute(block, axis, [(i, (i + shift) % n) for i in range(n)])


def gather_rows(block):
    n = lax.axis_size("zh")
    pieces = [block] + [shifted(block, "zh", k) for k in range(1, n)]
    block = jnp.concatenate(pieces, axis=1)
    for axis in ("y", "core"):
        block = lax.all_gather(block, axis, axis=1, tiled=True)
    return block


def scatter_rows(block):
    for axis in ("core", "y"):
        block = lax.psum_scatter(block, axis, scatter_dimension=0, tiled=True)
    n = lax.axis_size("zh")
    chunks = jnp.split(block, n, axis=0)
    total = chunks[0]
    for k in range(1, n):
        total = total + shifted(chunks[k], "zh", -k)
    return total


def per_device(saved_input, grad_sent, kept_blocks, gate_blocks, up_blocks, down_blocks):
    width = saved_input.shape[2]
    block = gate_blocks.shape[2]
    bands = width // block
    n_dp = 1
    for axis in ROW_AXES:
        n_dp *= lax.axis_size(axis)
    columns = FF // n_dp // block
    ids = kept_blocks[0]
    band_ids = ids // columns
    col_ids = ids % columns
    w_gate = gate_blocks[0]
    w_up = up_blocks[0]
    w_down = down_blocks[0]
    col_onehot = (col_ids[:, None] == jnp.arange(columns, dtype=jnp.int32)[None, :]).astype(
        jnp.float32
    )
    band_onehot = (band_ids[:, None] == jnp.arange(bands, dtype=jnp.int32)[None, :]).astype(
        jnp.float32
    )

    def to_columns(partial_value):
        spread = jnp.einsum("tkc,kn->tnc", partial_value, col_onehot)
        return spread.reshape(partial_value.shape[0], columns * block)

    def pick_cols(values):
        return jnp.take(values.reshape(values.shape[0], columns, block), col_ids, axis=1)

    def pick_bands(values):
        return jnp.take(values.reshape(values.shape[0], bands, block), band_ids, axis=1)

    incoming = passed_along(grad_sent, "section", -1)
    both = gather_rows(jnp.concatenate([saved_input, incoming], axis=0))
    inputs = both[0]
    upstream = both[1]
    chosen = pick_bands(inputs)
    gate = to_columns(
        jnp.einsum("tkb,kbc->tkc", chosen, w_gate, preferred_element_type=jnp.float32)
    )
    up = to_columns(jnp.einsum("tkb,kbc->tkc", chosen, w_up, preferred_element_type=jnp.float32))
    sig = jax.nn.sigmoid(gate)
    act = gate * sig
    hidden = (act * up).astype(jnp.bfloat16)
    grad_sel = pick_bands(upstream)
    dhid = to_columns(
        jnp.einsum("tkb,kcb->tkc", grad_sel, w_down, preferred_element_type=jnp.float32)
    )
    grad_up_act = (dhid * act).astype(jnp.bfloat16)
    grad_gate_act = (dhid * up * sig * (1.0 + gate * (1.0 - sig))).astype(jnp.bfloat16)
    input_sel = chosen
    tiles_down = jnp.einsum(
        "tkc,tkb->kcb", pick_cols(hidden), grad_sel, preferred_element_type=jnp.float32
    )
    tiles_gate = jnp.einsum(
        "tkb,tkc->kbc", input_sel, pick_cols(grad_gate_act), preferred_element_type=jnp.float32
    )
    tiles_up = jnp.einsum(
        "tkb,tkc->kbc", input_sel, pick_cols(grad_up_act), preferred_element_type=jnp.float32
    )
    slots = jnp.einsum(
        "tkc,kbc->tkb", pick_cols(grad_gate_act), w_gate, preferred_element_type=jnp.float32
    )
    slots = slots + jnp.einsum(
        "tkc,kbc->tkb", pick_cols(grad_up_act), w_up, preferred_element_type=jnp.float32
    )
    spread = jnp.einsum("tkb,kr->trb", slots, band_onehot)
    whole_term = spread.reshape(grad_gate_act.shape[0], bands * block)
    summed = scatter_rows(whole_term)
    grad_input = summed.astype(jnp.bfloat16)[None]
    return (
        grad_input,
        tiles_gate.astype(jnp.bfloat16)[None],
        tiles_up.astype(jnp.bfloat16)[None],
        tiles_down.astype(jnp.bfloat16)[None],
    )


def solution(mesh):
    n_dp = mesh.shape["dp"]
    split = Mesh(
        mesh.devices.reshape(mesh.shape["section"], n_dp // 8, 4, 2),
        ("section",) + ROW_AXES,
    )
    rows = P("section", ROW_AXES, None)
    blocks = P("section", ROW_AXES, None, None)
    return jax.shard_map(
        per_device,
        mesh=split,
        in_specs=(rows, rows, P("section", ROW_AXES), blocks, blocks, blocks),
        out_specs=(rows, blocks, blocks, blocks),
        check_vma=False,
    )
```

```python
import jax
import jax.numpy as jnp
from jax import lax
from jax.sharding import Mesh, PartitionSpec as P

FF = 16384
ROW_AXES = ("y", "zh", "core")


def passed_along(block, axis, distance):
    devices = range(lax.axis_size(axis))
    route = [((i - distance) % len(devices), i) for i in devices]
    return lax.ppermute(block, axis, route)


def shifted(block, axis, shift):
    n = lax.axis_size(axis)
    return lax.ppermute(block, axis, [(i, (i + shift) % n) for i in range(n)])


def shifted(block, axis, shift):
    n = lax.axis_size(axis)
    return lax.ppermute(block, axis, [(i, (i + shift) % n) for i in range(n)])


def gather_rows(block):
    for axis in (("y", "zh"), "core"):
        block = lax.all_gather(block, axis, axis=1, tiled=True)
    return block


def scatter_rows(block):
    for axis in ("core", "y"):
        block = lax.psum_scatter(block, axis, scatter_dimension=0, tiled=True)
    n = lax.axis_size("zh")
    idx = lax.axis_index("zh")
    chunks = jnp.split(block, n, axis=0)
    total = None
    for k in range(1, n):
        sent = jnp.stack(chunks)[(idx - k) % n]
        got = shifted(sent, "zh", -k)
        total = got if total is None else total + got
    return total + jnp.stack(chunks)[idx]


def per_device(saved_input, grad_sent, kept_blocks, gate_blocks, up_blocks, down_blocks):
    width = saved_input.shape[2]
    block = gate_blocks.shape[2]
    bands = width // block
    n_dp = 1
    for axis in ROW_AXES:
        n_dp *= lax.axis_size(axis)
    columns = FF // n_dp // block
    ids = kept_blocks[0]
    band_ids = ids // columns
    col_ids = ids % columns
    w_gate = gate_blocks[0]
    w_up = up_blocks[0]
    w_down = down_blocks[0]
    col_onehot = (col_ids[:, None] == jnp.arange(columns, dtype=jnp.int32)[None, :]).astype(
        jnp.float32
    )
    band_onehot = (band_ids[:, None] == jnp.arange(bands, dtype=jnp.int32)[None, :]).astype(
        jnp.float32
    )

    def to_columns(partial_value):
        spread = jnp.einsum("tkc,kn->tnc", partial_value, col_onehot)
        return spread.reshape(partial_value.shape[0], columns * block)

    def pick_cols(values):
        return jnp.take(values.reshape(values.shape[0], columns, block), col_ids, axis=1)

    def pick_bands(values):
        return jnp.take(values.reshape(values.shape[0], bands, block), band_ids, axis=1)

    incoming = passed_along(grad_sent, "section", -1)
    both = gather_rows(jnp.concatenate([saved_input, incoming], axis=0))
    inputs = both[0]
    upstream = both[1]
    chosen = pick_bands(inputs)
    gate = to_columns(
        jnp.einsum("tkb,kbc->tkc", chosen, w_gate, preferred_element_type=jnp.float32)
    )
    up = to_columns(jnp.einsum("tkb,kbc->tkc", chosen, w_up, preferred_element_type=jnp.float32))
    sig = jax.nn.sigmoid(gate)
    act = gate * sig
    hidden = (act * up).astype(jnp.bfloat16)
    grad_sel = pick_bands(upstream)
    dhid = to_columns(
        jnp.einsum("tkb,kcb->tkc", grad_sel, w_down, preferred_element_type=jnp.float32)
    )
    grad_up_act = (dhid * act).astype(jnp.bfloat16)
    grad_gate_act = (dhid * up * sig * (1.0 + gate * (1.0 - sig))).astype(jnp.bfloat16)
    input_sel = chosen
    tiles_down = jnp.einsum(
        "tkc,tkb->kcb", pick_cols(hidden), grad_sel, preferred_element_type=jnp.float32
    )
    tiles_gate = jnp.einsum(
        "tkb,tkc->kbc", input_sel, pick_cols(grad_gate_act), preferred_element_type=jnp.float32
    )
    tiles_up = jnp.einsum(
        "tkb,tkc->kbc", input_sel, pick_cols(grad_up_act), preferred_element_type=jnp.float32
    )
    slots = jnp.einsum(
        "tkc,kbc->tkb", pick_cols(grad_gate_act), w_gate, preferred_element_type=jnp.float32
    )
    slots = slots + jnp.einsum(
        "tkc,kbc->tkb", pick_cols(grad_up_act), w_up, preferred_element_type=jnp.float32
    )
    spread = jnp.einsum("tkb,kr->trb", slots, band_onehot)
    whole_term = spread.reshape(grad_gate_act.shape[0], bands * block)
    summed = scatter_rows(whole_term)
    grad_input = summed.astype(jnp.bfloat16)[None]
    return (
        grad_input,
        tiles_gate.astype(jnp.bfloat16)[None],
        tiles_up.astype(jnp.bfloat16)[None],
        tiles_down.astype(jnp.bfloat16)[None],
    )


def solution(mesh):
    n_dp = mesh.shape["dp"]
    split = Mesh(
        mesh.devices.reshape(mesh.shape["section"], n_dp // 8, 4, 2),
        ("section",) + ROW_AXES,
    )
    rows = P("section", ROW_AXES, None)
    blocks = P("section", ROW_AXES, None, None)
    return jax.shard_map(
        per_device,
        mesh=split,
        in_specs=(rows, rows, P("section", ROW_AXES), blocks, blocks, blocks),
        out_specs=(rows, blocks, blocks, blocks),
        check_vma=False,
    )
```

```python
import jax
import jax.numpy as jnp
from jax import lax
from jax.sharding import Mesh, PartitionSpec as P

FF = 16384
ROW_AXES = ("y", "zh", "core")


def passed_along(block, axis, distance):
    devices = range(lax.axis_size(axis))
    route = [((i - distance) % len(devices), i) for i in devices]
    return lax.ppermute(block, axis, route)


def shifted(block, axis, shift):
    n = lax.axis_size(axis)
    return lax.ppermute(block, axis, [(i, (i + shift) % n) for i in range(n)])


def gather_rows(block):
    n = lax.axis_size("zh")
    pieces = [block] + [shifted(block, "zh", k) for k in range(1, n)]
    block = jnp.concatenate(pieces, axis=1)
    for axis in ("y", "core"):
        block = lax.all_gather(block, axis, axis=1, tiled=True)
    return block


def scatter_rows(block):
    block = block.astype(jnp.bfloat16)
    for axis in ("core", "y"):
        block = lax.psum_scatter(block, axis, scatter_dimension=0, tiled=True)
    n = lax.axis_size("zh")
    chunks = jnp.split(block, n, axis=0)
    total = chunks[0].astype(jnp.float32)
    for k in range(1, n):
        total = total + shifted(chunks[k], "zh", -k).astype(jnp.float32)
    return total


def per_device(saved_input, grad_sent, kept_blocks, gate_blocks, up_blocks, down_blocks):
    width = saved_input.shape[2]
    block = gate_blocks.shape[2]
    bands = width // block
    n_dp = 1
    for axis in ROW_AXES:
        n_dp *= lax.axis_size(axis)
    columns = FF // n_dp // block
    ids = kept_blocks[0]
    band_ids = ids // columns
    col_ids = ids % columns
    w_gate = gate_blocks[0]
    w_up = up_blocks[0]
    w_down = down_blocks[0]
    col_onehot = (col_ids[:, None] == jnp.arange(columns, dtype=jnp.int32)[None, :]).astype(
        jnp.float32
    )
    band_onehot = (band_ids[:, None] == jnp.arange(bands, dtype=jnp.int32)[None, :]).astype(
        jnp.float32
    )

    def to_columns(partial_value):
        spread = jnp.einsum("tkc,kn->tnc", partial_value, col_onehot)
        return spread.reshape(partial_value.shape[0], columns * block)

    def pick_cols(values):
        return jnp.take(values.reshape(values.shape[0], columns, block), col_ids, axis=1)

    def pick_bands(values):
        return jnp.take(values.reshape(values.shape[0], bands, block), band_ids, axis=1)

    incoming = passed_along(grad_sent, "section", -1)
    both = gather_rows(jnp.concatenate([saved_input, incoming], axis=0))
    inputs = both[0]
    upstream = both[1]
    chosen = pick_bands(inputs)
    gate = to_columns(
        jnp.einsum("tkb,kbc->tkc", chosen, w_gate, preferred_element_type=jnp.float32)
    )
    up = to_columns(jnp.einsum("tkb,kbc->tkc", chosen, w_up, preferred_element_type=jnp.float32))
    sig = jax.nn.sigmoid(gate)
    act = gate * sig
    hidden = (act * up).astype(jnp.bfloat16)
    grad_sel = pick_bands(upstream)
    dhid = to_columns(
        jnp.einsum("tkb,kcb->tkc", grad_sel, w_down, preferred_element_type=jnp.float32)
    )
    grad_up_act = (dhid * act).astype(jnp.bfloat16)
    grad_gate_act = (dhid * up * sig * (1.0 + gate * (1.0 - sig))).astype(jnp.bfloat16)
    input_sel = chosen
    tiles_down = jnp.einsum(
        "tkc,tkb->kcb", pick_cols(hidden), grad_sel, preferred_element_type=jnp.float32
    )
    tiles_gate = jnp.einsum(
        "tkb,tkc->kbc", input_sel, pick_cols(grad_gate_act), preferred_element_type=jnp.float32
    )
    tiles_up = jnp.einsum(
        "tkb,tkc->kbc", input_sel, pick_cols(grad_up_act), preferred_element_type=jnp.float32
    )
    slots = jnp.einsum(
        "tkc,kbc->tkb", pick_cols(grad_gate_act), w_gate, preferred_element_type=jnp.float32
    )
    slots = slots + jnp.einsum(
        "tkc,kbc->tkb", pick_cols(grad_up_act), w_up, preferred_element_type=jnp.float32
    )
    spread = jnp.einsum("tkb,kr->trb", slots, band_onehot)
    whole_term = spread.reshape(grad_gate_act.shape[0], bands * block)
    summed = scatter_rows(whole_term)
    grad_input = summed.astype(jnp.bfloat16)[None]
    return (
        grad_input,
        tiles_gate.astype(jnp.bfloat16)[None],
        tiles_up.astype(jnp.bfloat16)[None],
        tiles_down.astype(jnp.bfloat16)[None],
    )


def solution(mesh):
    n_dp = mesh.shape["dp"]
    split = Mesh(
        mesh.devices.reshape(mesh.shape["section"], n_dp // 8, 4, 2),
        ("section",) + ROW_AXES,
    )
    rows = P("section", ROW_AXES, None)
    blocks = P("section", ROW_AXES, None, None)
    return jax.shard_map(
        per_device,
        mesh=split,
        in_specs=(rows, rows, P("section", ROW_AXES), blocks, blocks, blocks),
        out_specs=(rows, blocks, blocks, blocks),
        check_vma=False,
    )
```

```python
import jax
import jax.numpy as jnp
from jax import lax
from jax.sharding import Mesh, PartitionSpec as P

FF = 16384
ROW_AXES = ("y", "zh", "core")


def passed_along(block, axis, distance):
    devices = range(lax.axis_size(axis))
    route = [((i - distance) % len(devices), i) for i in devices]
    return lax.ppermute(block, axis, route)


def shifted(block, axis, shift):
    n = lax.axis_size(axis)
    return lax.ppermute(block, axis, [(i, (i + shift) % n) for i in range(n)])


def gather_rows(block):
    n = lax.axis_size("zh")
    pieces = [block] + [shifted(block, "zh", k) for k in range(1, n)]
    block = jnp.concatenate(pieces, axis=1)
    block = lax.all_gather(block, "y", axis=1, tiled=True)
    return jnp.concatenate([block, shifted(block, "core", 1)], axis=1)


def scatter_rows(block):
    own, other = jnp.split(block, 2, axis=0)
    block = (own + shifted(other, "core", 1)).astype(jnp.bfloat16)
    block = lax.psum_scatter(block, "y", scatter_dimension=0, tiled=True)
    n = lax.axis_size("zh")
    chunks = jnp.split(block, n, axis=0)
    total = chunks[0].astype(jnp.float32)
    for k in range(1, n):
        total = total + shifted(chunks[k], "zh", -k).astype(jnp.float32)
    return total


def per_device(saved_input, grad_sent, kept_blocks, gate_blocks, up_blocks, down_blocks):
    width = saved_input.shape[2]
    block = gate_blocks.shape[2]
    bands = width // block
    n_dp = 1
    for axis in ROW_AXES:
        n_dp *= lax.axis_size(axis)
    columns = FF // n_dp // block
    ids = kept_blocks[0]
    band_ids = ids // columns
    col_ids = ids % columns
    w_gate = gate_blocks[0]
    w_up = up_blocks[0]
    w_down = down_blocks[0]
    col_onehot = (col_ids[:, None] == jnp.arange(columns, dtype=jnp.int32)[None, :]).astype(
        jnp.float32
    )
    band_onehot = (band_ids[:, None] == jnp.arange(bands, dtype=jnp.int32)[None, :]).astype(
        jnp.float32
    )

    def to_columns(partial_value):
        spread = jnp.einsum("tkc,kn->tnc", partial_value, col_onehot)
        return spread.reshape(partial_value.shape[0], columns * block)

    def pick_cols(values):
        return jnp.take(values.reshape(values.shape[0], columns, block), col_ids, axis=1)

    def pick_bands(values):
        return jnp.take(values.reshape(values.shape[0], bands, block), band_ids, axis=1)

    incoming = passed_along(grad_sent, "section", -1)
    both = gather_rows(jnp.concatenate([saved_input, incoming], axis=0))
    inputs = both[0]
    upstream = both[1]
    chosen = pick_bands(inputs)
    gate = to_columns(
        jnp.einsum("tkb,kbc->tkc", chosen, w_gate, preferred_element_type=jnp.float32)
    )
    up = to_columns(jnp.einsum("tkb,kbc->tkc", chosen, w_up, preferred_element_type=jnp.float32))
    sig = jax.nn.sigmoid(gate)
    act = gate * sig
    hidden = (act * up).astype(jnp.bfloat16)
    grad_sel = pick_bands(upstream)
    dhid = to_columns(
        jnp.einsum("tkb,kcb->tkc", grad_sel, w_down, preferred_element_type=jnp.float32)
    )
    grad_up_act = (dhid * act).astype(jnp.bfloat16)
    grad_gate_act = (dhid * up * sig * (1.0 + gate * (1.0 - sig))).astype(jnp.bfloat16)
    input_sel = chosen
    tiles_down = jnp.einsum(
        "tkc,tkb->kcb", pick_cols(hidden), grad_sel, preferred_element_type=jnp.float32
    )
    tiles_gate = jnp.einsum(
        "tkb,tkc->kbc", input_sel, pick_cols(grad_gate_act), preferred_element_type=jnp.float32
    )
    tiles_up = jnp.einsum(
        "tkb,tkc->kbc", input_sel, pick_cols(grad_up_act), preferred_element_type=jnp.float32
    )
    slots = jnp.einsum(
        "tkc,kbc->tkb", pick_cols(grad_gate_act), w_gate, preferred_element_type=jnp.float32
    )
    slots = slots + jnp.einsum(
        "tkc,kbc->tkb", pick_cols(grad_up_act), w_up, preferred_element_type=jnp.float32
    )
    spread = jnp.einsum("tkb,kr->trb", slots, band_onehot)
    whole_term = spread.reshape(grad_gate_act.shape[0], bands * block)
    summed = scatter_rows(whole_term)
    grad_input = summed.astype(jnp.bfloat16)[None]
    return (
        grad_input,
        tiles_gate.astype(jnp.bfloat16)[None],
        tiles_up.astype(jnp.bfloat16)[None],
        tiles_down.astype(jnp.bfloat16)[None],
    )


def solution(mesh):
    n_dp = mesh.shape["dp"]
    split = Mesh(
        mesh.devices.reshape(mesh.shape["section"], n_dp // 8, 4, 2),
        ("section",) + ROW_AXES,
    )
    rows = P("section", ROW_AXES, None)
    blocks = P("section", ROW_AXES, None, None)
    return jax.shard_map(
        per_device,
        mesh=split,
        in_specs=(rows, rows, P("section", ROW_AXES), blocks, blocks, blocks),
        out_specs=(rows, blocks, blocks, blocks),
        check_vma=False,
    )
```

```python
import jax
import jax.numpy as jnp
from jax import lax
from jax.sharding import Mesh, PartitionSpec as P

FF = 16384
ROW_AXES = ("y", "zh", "core")


def passed_along(block, axis, distance):
    devices = range(lax.axis_size(axis))
    route = [((i - distance) % len(devices), i) for i in devices]
    return lax.ppermute(block, axis, route)


def shifted(block, axis, shift):
    n = lax.axis_size(axis)
    return lax.ppermute(block, axis, [(i, (i + shift) % n) for i in range(n)])


def gather_rows(block):
    n = lax.axis_size("zh")
    pieces = [block] + [shifted(block, "zh", k) for k in range(1, n)]
    block = jnp.concatenate(pieces, axis=1)
    block = lax.all_gather(block, "y", axis=1, tiled=True)
    return jnp.concatenate([block, shifted(block, "core", 1)], axis=1)


def scatter_rows(block):
    own, other = jnp.split(block, 2, axis=0)
    block = (own + shifted(other, "core", 1)).astype(jnp.bfloat16)
    block = lax.psum_scatter(block, "y", scatter_dimension=0, tiled=True)
    n = lax.axis_size("zh")
    chunks = jnp.split(block, n, axis=0)
    total = chunks[0].astype(jnp.float32)
    for k in range(1, n):
        total = total + shifted(chunks[k], "zh", -k).astype(jnp.float32)
    return total


def per_device(saved_input, grad_sent, kept_blocks, gate_blocks, up_blocks, down_blocks):
    width = saved_input.shape[2]
    block = gate_blocks.shape[2]
    bands = width // block
    n_dp = 1
    for axis in ROW_AXES:
        n_dp *= lax.axis_size(axis)
    columns = FF // n_dp // block
    ids = kept_blocks[0]
    band_ids = ids // columns
    col_ids = ids % columns
    band_onehot = (band_ids[:, None] == jnp.arange(bands, dtype=jnp.int32)[None, :]).astype(
        jnp.bfloat16
    )
    col_onehot = (col_ids[:, None] == jnp.arange(columns, dtype=jnp.int32)[None, :]).astype(
        jnp.bfloat16
    )
    hidden_units = columns * block

    def dense_in(blocks):
        placed = jnp.einsum(
            "kr,kc,kbn->rbcn", band_onehot, col_onehot, blocks,
            preferred_element_type=jnp.float32,
        )
        return placed.astype(jnp.bfloat16).reshape(width, hidden_units)

    def dense_down(blocks):
        placed = jnp.einsum(
            "kc,kr,knb->cnrb", col_onehot, band_onehot, blocks,
            preferred_element_type=jnp.float32,
        )
        return placed.astype(jnp.bfloat16).reshape(hidden_units, width)

    def kept_in(dense):
        tiles = dense.astype(jnp.bfloat16).reshape(bands, block, columns, block)
        picked = jnp.einsum(
            "kr,kc,rbcn->kbn", band_onehot, col_onehot, tiles,
            preferred_element_type=jnp.float32,
        )
        return picked.astype(jnp.bfloat16)

    def kept_down(dense):
        tiles = dense.astype(jnp.bfloat16).reshape(columns, block, bands, block)
        picked = jnp.einsum(
            "kc,kr,cnrb->knb", col_onehot, band_onehot, tiles,
            preferred_element_type=jnp.float32,
        )
        return picked.astype(jnp.bfloat16)

    w_gate = dense_in(gate_blocks[0])
    w_up = dense_in(up_blocks[0])
    w_down = dense_down(down_blocks[0])

    incoming = passed_along(grad_sent, "section", -1)
    both = gather_rows(jnp.concatenate([saved_input, incoming], axis=0))
    inputs = both[0]
    upstream = both[1]
    f32 = jnp.float32
    gate = jnp.dot(inputs, w_gate, preferred_element_type=f32)
    up = jnp.dot(inputs, w_up, preferred_element_type=f32)
    sig = jax.nn.sigmoid(gate)
    act = gate * sig
    hidden = (act * up).astype(jnp.bfloat16)
    dhid = lax.dot_general(upstream, w_down, (((1,), (1,)), ((), ())), preferred_element_type=f32)
    grad_up_act = (dhid * act).astype(jnp.bfloat16)
    grad_gate_act = (dhid * up * sig * (1.0 + gate * (1.0 - sig))).astype(jnp.bfloat16)
    rows_t = (((0,), (0,)), ((), ()))
    tiles_gate = kept_in(lax.dot_general(inputs, grad_gate_act, rows_t, preferred_element_type=f32))
    tiles_up = kept_in(lax.dot_general(inputs, grad_up_act, rows_t, preferred_element_type=f32))
    tiles_down = kept_down(lax.dot_general(hidden, upstream, rows_t, preferred_element_type=f32))
    hid_t = (((1,), (1,)), ((), ()))
    whole_term = lax.dot_general(grad_gate_act, w_gate, hid_t, preferred_element_type=f32)
    whole_term = whole_term + lax.dot_general(
        grad_up_act, w_up, hid_t, preferred_element_type=f32
    )
    summed = scatter_rows(whole_term)
    grad_input = summed.astype(jnp.bfloat16)[None]
    return (grad_input, tiles_gate[None], tiles_up[None], tiles_down[None])


def solution(mesh):
    n_dp = mesh.shape["dp"]
    split = Mesh(
        mesh.devices.reshape(mesh.shape["section"], n_dp // 8, 4, 2),
        ("section",) + ROW_AXES,
    )
    rows = P("section", ROW_AXES, None)
    blocks = P("section", ROW_AXES, None, None)
    return jax.shard_map(
        per_device,
        mesh=split,
        in_specs=(rows, rows, P("section", ROW_AXES), blocks, blocks, blocks),
        out_specs=(rows, blocks, blocks, blocks),
        check_vma=False,
    )
```

```python
import jax
import jax.numpy as jnp
from jax import lax
from jax.sharding import Mesh, PartitionSpec as P

FF = 16384
ROW_AXES = ("y", "zh", "core")


def passed_along(block, axis, distance):
    devices = range(lax.axis_size(axis))
    route = [((i - distance) % len(devices), i) for i in devices]
    return lax.ppermute(block, axis, route)


def shifted(block, axis, shift):
    n = lax.axis_size(axis)
    return lax.ppermute(block, axis, [(i, (i + shift) % n) for i in range(n)])


def gather_rows(block, weights):
    n = lax.axis_size("zh")
    pieces = [block] + [shifted(block, "zh", k) for k in range(1, n)]
    block = jnp.concatenate(pieces, axis=1)
    block, weights = lax.optimization_barrier((block, weights))
    block = lax.all_gather(block, "y", axis=1, tiled=True)
    return jnp.concatenate([block, shifted(block, "core", 1)], axis=1), weights


def scatter_rows(block):
    own, other = jnp.split(block, 2, axis=0)
    block = (own + shifted(other, "core", 1)).astype(jnp.bfloat16)
    block = lax.psum_scatter(block, "y", scatter_dimension=0, tiled=True)
    n = lax.axis_size("zh")
    chunks = jnp.split(block, n, axis=0)
    total = chunks[0].astype(jnp.float32)
    for k in range(1, n):
        total = total + shifted(chunks[k], "zh", -k).astype(jnp.float32)
    return total


def per_device(saved_input, grad_sent, kept_blocks, gate_blocks, up_blocks, down_blocks):
    width = saved_input.shape[2]
    block = gate_blocks.shape[2]
    bands = width // block
    n_dp = 1
    for axis in ROW_AXES:
        n_dp *= lax.axis_size(axis)
    columns = FF // n_dp // block
    ids = kept_blocks[0]
    band_ids = ids // columns
    col_ids = ids % columns
    band_onehot = (band_ids[:, None] == jnp.arange(bands, dtype=jnp.int32)[None, :]).astype(
        jnp.bfloat16
    )
    col_onehot = (col_ids[:, None] == jnp.arange(columns, dtype=jnp.int32)[None, :]).astype(
        jnp.bfloat16
    )
    hidden_units = columns * block

    def dense_in(blocks):
        spread = blocks[:, :, None, :] * col_onehot[:, None, :, None]
        placed = lax.dot_general(
            band_onehot, spread, (((0,), (0,)), ((), ())), preferred_element_type=jnp.float32
        )
        return placed.astype(jnp.bfloat16).reshape(width, hidden_units)

    def kept_in(dense):
        tiles = dense.astype(jnp.bfloat16).reshape(bands, block * columns * block)
        picked = jnp.dot(band_onehot, tiles, preferred_element_type=jnp.float32)
        picked = picked.reshape(-1, block, columns, block) * col_onehot[:, None, :, None]
        return jnp.sum(picked, axis=2).astype(jnp.bfloat16)

    w_gate = dense_in(gate_blocks[0])
    w_up = dense_in(up_blocks[0])
    w_down_t = dense_in(jnp.swapaxes(down_blocks[0], 1, 2))

    incoming = passed_along(grad_sent, "section", -1)
    both, (w_gate, w_up, w_down_t) = gather_rows(
        jnp.concatenate([saved_input, incoming], axis=0), (w_gate, w_up, w_down_t)
    )
    inputs = both[0]
    upstream = both[1]
    f32 = jnp.float32
    gate = jnp.dot(inputs, w_gate, preferred_element_type=f32)
    up = jnp.dot(inputs, w_up, preferred_element_type=f32)
    sig = jax.nn.sigmoid(gate)
    act = gate * sig
    hidden = (act * up).astype(jnp.bfloat16)
    dhid = jnp.dot(upstream, w_down_t, preferred_element_type=f32)
    grad_up_act = (dhid * act).astype(jnp.bfloat16)
    grad_gate_act = (dhid * up * sig * (1.0 + gate * (1.0 - sig))).astype(jnp.bfloat16)
    rows_t = (((0,), (0,)), ((), ()))
    tiles_gate = kept_in(lax.dot_general(inputs, grad_gate_act, rows_t, preferred_element_type=f32))
    tiles_up = kept_in(lax.dot_general(inputs, grad_up_act, rows_t, preferred_element_type=f32))
    tiles_down = jnp.swapaxes(
        kept_in(lax.dot_general(upstream, hidden, rows_t, preferred_element_type=f32)), 1, 2
    )
    hid_t = (((1,), (1,)), ((), ()))
    whole_term = lax.dot_general(grad_gate_act, w_gate, hid_t, preferred_element_type=f32)
    whole_term = whole_term + lax.dot_general(
        grad_up_act, w_up, hid_t, preferred_element_type=f32
    )
    summed = scatter_rows(whole_term)
    grad_input = summed.astype(jnp.bfloat16)[None]
    return (grad_input, tiles_gate[None], tiles_up[None], tiles_down[None])


def solution(mesh):
    n_dp = mesh.shape["dp"]
    split = Mesh(
        mesh.devices.reshape(mesh.shape["section"], n_dp // 8, 4, 2),
        ("section",) + ROW_AXES,
    )
    rows = P("section", ROW_AXES, None)
    blocks = P("section", ROW_AXES, None, None)
    return jax.shard_map(
        per_device,
        mesh=split,
        in_specs=(rows, rows, P("section", ROW_AXES), blocks, blocks, blocks),
        out_specs=(rows, blocks, blocks, blocks),
        check_vma=False,
    )
```

```python
import jax
import jax.numpy as jnp
from jax import lax
from jax.sharding import Mesh, PartitionSpec as P

FF = 16384
ROW_AXES = ("y", "zh", "core")


def passed_along(block, axis, distance):
    devices = range(lax.axis_size(axis))
    route = [((i - distance) % len(devices), i) for i in devices]
    return lax.ppermute(block, axis, route)


def shifted(block, axis, shift):
    n = lax.axis_size(axis)
    return lax.ppermute(block, axis, [(i, (i + shift) % n) for i in range(n)])


def gather_rows(block, weights):
    n = lax.axis_size("zh")
    pieces = [block] + [shifted(block, "zh", k) for k in range(1, n)]
    block = jnp.concatenate(pieces, axis=1)
    block = lax.all_gather(block, "y", axis=1, tiled=True)
    block, weights = lax.optimization_barrier((block, weights))
    return jnp.concatenate([block, shifted(block, "core", 1)], axis=1), weights


def scatter_rows(block):
    own, other = jnp.split(block, 2, axis=0)
    block = (own + shifted(other, "core", 1)).astype(jnp.bfloat16)
    block = lax.psum_scatter(block, "y", scatter_dimension=0, tiled=True)
    n = lax.axis_size("zh")
    chunks = jnp.split(block, n, axis=0)
    total = chunks[0].astype(jnp.float32)
    for k in range(1, n):
        total = total + shifted(chunks[k], "zh", -k).astype(jnp.float32)
    return total


def per_device(saved_input, grad_sent, kept_blocks, gate_blocks, up_blocks, down_blocks):
    width = saved_input.shape[2]
    block = gate_blocks.shape[2]
    bands = width // block
    n_dp = 1
    for axis in ROW_AXES:
        n_dp *= lax.axis_size(axis)
    columns = FF // n_dp // block
    ids = kept_blocks[0]
    band_ids = ids // columns
    col_ids = ids % columns
    band_onehot = (band_ids[:, None] == jnp.arange(bands, dtype=jnp.int32)[None, :]).astype(
        jnp.bfloat16
    )
    col_onehot = (col_ids[:, None] == jnp.arange(columns, dtype=jnp.int32)[None, :]).astype(
        jnp.bfloat16
    )
    hidden_units = columns * block

    def dense_in(blocks):
        placed = jnp.einsum(
            "kr,kc,kbn->rbcn", band_onehot, col_onehot, blocks,
            preferred_element_type=jnp.float32,
        )
        return placed.astype(jnp.bfloat16).reshape(width, hidden_units)

    def dense_down(blocks):
        placed = jnp.einsum(
            "kc,kr,knb->cnrb", col_onehot, band_onehot, blocks,
            preferred_element_type=jnp.float32,
        )
        return placed.astype(jnp.bfloat16).reshape(hidden_units, width)

    def kept_in(dense):
        tiles = dense.astype(jnp.bfloat16).reshape(bands, block, columns, block)
        picked = jnp.einsum(
            "kr,kc,rbcn->kbn", band_onehot, col_onehot, tiles,
            preferred_element_type=jnp.float32,
        )
        return picked.astype(jnp.bfloat16)

    def kept_down(dense):
        tiles = dense.astype(jnp.bfloat16).reshape(columns, block, bands, block)
        picked = jnp.einsum(
            "kc,kr,cnrb->knb", col_onehot, band_onehot, tiles,
            preferred_element_type=jnp.float32,
        )
        return picked.astype(jnp.bfloat16)

    w_gate = dense_in(gate_blocks[0])
    w_up = dense_in(up_blocks[0])
    w_down = dense_down(down_blocks[0])

    incoming = passed_along(grad_sent, "section", -1)
    both, (w_gate, w_up, w_down) = gather_rows(
        jnp.concatenate([saved_input, incoming], axis=0), (w_gate, w_up, w_down)
    )
    inputs = both[0]
    upstream = both[1]
    f32 = jnp.float32
    gate = jnp.dot(inputs, w_gate, preferred_element_type=f32)
    up = jnp.dot(inputs, w_up, preferred_element_type=f32)
    sig = jax.nn.sigmoid(gate)
    act = gate * sig
    hidden = (act * up).astype(jnp.bfloat16)
    dhid = lax.dot_general(upstream, w_down, (((1,), (1,)), ((), ())), preferred_element_type=f32)
    grad_up_act = (dhid * act).astype(jnp.bfloat16)
    grad_gate_act = (dhid * up * sig * (1.0 + gate * (1.0 - sig))).astype(jnp.bfloat16)
    rows_t = (((0,), (0,)), ((), ()))
    tiles_gate = kept_in(lax.dot_general(inputs, grad_gate_act, rows_t, preferred_element_type=f32))
    tiles_up = kept_in(lax.dot_general(inputs, grad_up_act, rows_t, preferred_element_type=f32))
    tiles_down = kept_down(lax.dot_general(hidden, upstream, rows_t, preferred_element_type=f32))
    hid_t = (((1,), (1,)), ((), ()))
    whole_term = lax.dot_general(grad_gate_act, w_gate, hid_t, preferred_element_type=f32)
    whole_term = whole_term + lax.dot_general(
        grad_up_act, w_up, hid_t, preferred_element_type=f32
    )
    summed = scatter_rows(whole_term)
    grad_input = summed.astype(jnp.bfloat16)[None]
    return (grad_input, tiles_gate[None], tiles_up[None], tiles_down[None])


def solution(mesh):
    n_dp = mesh.shape["dp"]
    split = Mesh(
        mesh.devices.reshape(mesh.shape["section"], n_dp // 8, 4, 2),
        ("section",) + ROW_AXES,
    )
    rows = P("section", ROW_AXES, None)
    blocks = P("section", ROW_AXES, None, None)
    return jax.shard_map(
        per_device,
        mesh=split,
        in_specs=(rows, rows, P("section", ROW_AXES), blocks, blocks, blocks),
        out_specs=(rows, blocks, blocks, blocks),
        check_vma=False,
    )
```

```python
import jax
import jax.numpy as jnp
from jax import lax
from jax.sharding import Mesh, PartitionSpec as P

FF = 16384
ROW_AXES = ("y", "zh", "core")


def passed_along(block, axis, distance):
    devices = range(lax.axis_size(axis))
    route = [((i - distance) % len(devices), i) for i in devices]
    return lax.ppermute(block, axis, route)


def shifted(block, axis, shift):
    n = lax.axis_size(axis)
    return lax.ppermute(block, axis, [(i, (i + shift) % n) for i in range(n)])


def gather_rows(block, weights):
    n = lax.axis_size("zh")
    copies = jnp.broadcast_to(block[None], (n,) + block.shape)
    block = lax.all_to_all(copies, "zh", 0, 0, tiled=True)
    block = jnp.swapaxes(block, 0, 1).reshape(block.shape[1], -1, block.shape[3])
    block = lax.all_gather(block, "y", axis=1, tiled=True)
    block, weights = lax.optimization_barrier((block, weights))
    return jnp.concatenate([block, shifted(block, "core", 1)], axis=1), weights


def scatter_rows(block):
    own, other = jnp.split(block, 2, axis=0)
    block = (own + shifted(other, "core", 1)).astype(jnp.bfloat16)
    block = lax.psum_scatter(block, "y", scatter_dimension=0, tiled=True)
    n = lax.axis_size("zh")
    chunks = block.reshape(n, -1, block.shape[1])
    got = lax.all_to_all(chunks, "zh", 0, 0, tiled=True)
    return jnp.sum(got.astype(jnp.float32), axis=0)


def per_device(saved_input, grad_sent, kept_blocks, gate_blocks, up_blocks, down_blocks):
    width = saved_input.shape[2]
    block = gate_blocks.shape[2]
    bands = width // block
    n_dp = 1
    for axis in ROW_AXES:
        n_dp *= lax.axis_size(axis)
    columns = FF // n_dp // block
    ids = kept_blocks[0]
    band_ids = ids // columns
    col_ids = ids % columns
    band_onehot = (band_ids[:, None] == jnp.arange(bands, dtype=jnp.int32)[None, :]).astype(
        jnp.bfloat16
    )
    col_onehot = (col_ids[:, None] == jnp.arange(columns, dtype=jnp.int32)[None, :]).astype(
        jnp.bfloat16
    )
    hidden_units = columns * block

    def dense_in(blocks):
        placed = jnp.einsum(
            "kr,kc,kbn->rbcn", band_onehot, col_onehot, blocks,
            preferred_element_type=jnp.float32,
        )
        return placed.astype(jnp.bfloat16).reshape(width, hidden_units)

    def dense_down(blocks):
        placed = jnp.einsum(
            "kc,kr,knb->cnrb", col_onehot, band_onehot, blocks,
            preferred_element_type=jnp.float32,
        )
        return placed.astype(jnp.bfloat16).reshape(hidden_units, width)

    def kept_in(dense):
        tiles = dense.astype(jnp.bfloat16).reshape(bands, block, columns, block)
        picked = jnp.einsum(
            "kr,kc,rbcn->kbn", band_onehot, col_onehot, tiles,
            preferred_element_type=jnp.float32,
        )
        return picked.astype(jnp.bfloat16)

    def kept_down(dense):
        tiles = dense.astype(jnp.bfloat16).reshape(columns, block, bands, block)
        picked = jnp.einsum(
            "kc,kr,cnrb->knb", col_onehot, band_onehot, tiles,
            preferred_element_type=jnp.float32,
        )
        return picked.astype(jnp.bfloat16)

    w_gate = dense_in(gate_blocks[0])
    w_up = dense_in(up_blocks[0])
    w_down = dense_down(down_blocks[0])

    incoming = passed_along(grad_sent, "section", -1)
    both, (w_gate, w_up, w_down) = gather_rows(
        jnp.concatenate([saved_input, incoming], axis=0), (w_gate, w_up, w_down)
    )
    inputs = both[0]
    upstream = both[1]
    f32 = jnp.float32
    gate = jnp.dot(inputs, w_gate, preferred_element_type=f32)
    up = jnp.dot(inputs, w_up, preferred_element_type=f32)
    sig = jax.nn.sigmoid(gate)
    act = gate * sig
    hidden = (act * up).astype(jnp.bfloat16)
    dhid = lax.dot_general(upstream, w_down, (((1,), (1,)), ((), ())), preferred_element_type=f32)
    grad_up_act = (dhid * act).astype(jnp.bfloat16)
    grad_gate_act = (dhid * up * sig * (1.0 + gate * (1.0 - sig))).astype(jnp.bfloat16)
    rows_t = (((0,), (0,)), ((), ()))
    tiles_gate = kept_in(lax.dot_general(inputs, grad_gate_act, rows_t, preferred_element_type=f32))
    tiles_up = kept_in(lax.dot_general(inputs, grad_up_act, rows_t, preferred_element_type=f32))
    tiles_down = kept_down(lax.dot_general(hidden, upstream, rows_t, preferred_element_type=f32))
    hid_t = (((1,), (1,)), ((), ()))
    whole_term = lax.dot_general(grad_gate_act, w_gate, hid_t, preferred_element_type=f32)
    whole_term = whole_term + lax.dot_general(
        grad_up_act, w_up, hid_t, preferred_element_type=f32
    )
    summed = scatter_rows(whole_term)
    grad_input = summed.astype(jnp.bfloat16)[None]
    return (grad_input, tiles_gate[None], tiles_up[None], tiles_down[None])


def solution(mesh):
    n_dp = mesh.shape["dp"]
    split = Mesh(
        mesh.devices.reshape(mesh.shape["section"], n_dp // 8, 4, 2),
        ("section",) + ROW_AXES,
    )
    rows = P("section", ROW_AXES, None)
    blocks = P("section", ROW_AXES, None, None)
    return jax.shard_map(
        per_device,
        mesh=split,
        in_specs=(rows, rows, P("section", ROW_AXES), blocks, blocks, blocks),
        out_specs=(rows, blocks, blocks, blocks),
        check_vma=False,
    )
```

```python
import jax
import jax.numpy as jnp
from jax import lax
from jax.sharding import Mesh, PartitionSpec as P

FF = 16384
ROW_AXES = ("y", "zh", "core")


def passed_along(block, axis, distance):
    devices = range(lax.axis_size(axis))
    route = [((i - distance) % len(devices), i) for i in devices]
    return lax.ppermute(block, axis, route)


def shifted(block, axis, shift):
    n = lax.axis_size(axis)
    return lax.ppermute(block, axis, [(i, (i + shift) % n) for i in range(n)])


def gather_rows(block, weights):
    n = lax.axis_size("zh")
    copies = jnp.broadcast_to(block[None], (n,) + block.shape)
    block = lax.all_to_all(copies, "zh", 0, 0, tiled=True)
    block = jnp.swapaxes(block, 0, 1).reshape(block.shape[1], -1, block.shape[3])
    block = lax.all_gather(block, "y", axis=1, tiled=True)
    block, weights = lax.optimization_barrier((block, weights))
    return jnp.concatenate([block, shifted(block, "core", 1)], axis=1), weights


def ring_reduce(block, axis):
    n = lax.axis_size(axis)
    idx = lax.axis_index(axis)
    chunks = block.reshape(n, -1, block.shape[1])

    def chunk_for(dist):
        return lax.dynamic_index_in_dim(chunks, (idx + dist) % n, 0, keepdims=False)

    back = n // 2
    ahead = n - 1 - back
    acc = chunk_for(-back).astype(jnp.float32)
    for d in range(back - 1, -1, -1):
        acc = shifted(acc.astype(jnp.bfloat16), axis, -1).astype(jnp.float32) + chunk_for(-d)
    total = acc
    if ahead:
        acc = chunk_for(ahead).astype(jnp.float32)
        for d in range(ahead - 1, 0, -1):
            acc = shifted(acc.astype(jnp.bfloat16), axis, 1).astype(jnp.float32) + chunk_for(d)
        total = total + shifted(acc.astype(jnp.bfloat16), axis, 1).astype(jnp.float32)
    return total


def scatter_rows(block):
    own, other = jnp.split(block, 2, axis=0)
    block = own + shifted(other, "core", 1)
    block = ring_reduce(block, "y").astype(jnp.bfloat16)
    n = lax.axis_size("zh")
    chunks = block.reshape(n, -1, block.shape[1])
    got = lax.all_to_all(chunks, "zh", 0, 0, tiled=True)
    return jnp.sum(got.astype(jnp.float32), axis=0)


def per_device(saved_input, grad_sent, kept_blocks, gate_blocks, up_blocks, down_blocks):
    width = saved_input.shape[2]
    block = gate_blocks.shape[2]
    bands = width // block
    n_dp = 1
    for axis in ROW_AXES:
        n_dp *= lax.axis_size(axis)
    columns = FF // n_dp // block
    ids = kept_blocks[0]
    band_ids = ids // columns
    col_ids = ids % columns
    band_onehot = (band_ids[:, None] == jnp.arange(bands, dtype=jnp.int32)[None, :]).astype(
        jnp.bfloat16
    )
    col_onehot = (col_ids[:, None] == jnp.arange(columns, dtype=jnp.int32)[None, :]).astype(
        jnp.bfloat16
    )
    hidden_units = columns * block

    def dense_in(blocks):
        placed = jnp.einsum(
            "kr,kc,kbn->rbcn", band_onehot, col_onehot, blocks,
            preferred_element_type=jnp.float32,
        )
        return placed.astype(jnp.bfloat16).reshape(width, hidden_units)

    def dense_down(blocks):
        placed = jnp.einsum(
            "kc,kr,knb->cnrb", col_onehot, band_onehot, blocks,
            preferred_element_type=jnp.float32,
        )
        return placed.astype(jnp.bfloat16).reshape(hidden_units, width)

    def kept_in(dense):
        tiles = dense.astype(jnp.bfloat16).reshape(bands, block, columns, block)
        picked = jnp.einsum(
            "kr,kc,rbcn->kbn", band_onehot, col_onehot, tiles,
            preferred_element_type=jnp.float32,
        )
        return picked.astype(jnp.bfloat16)

    def kept_down(dense):
        tiles = dense.astype(jnp.bfloat16).reshape(columns, block, bands, block)
        picked = jnp.einsum(
            "kc,kr,cnrb->knb", col_onehot, band_onehot, tiles,
            preferred_element_type=jnp.float32,
        )
        return picked.astype(jnp.bfloat16)

    w_gate = dense_in(gate_blocks[0])
    w_up = dense_in(up_blocks[0])
    w_down = dense_down(down_blocks[0])

    incoming = passed_along(grad_sent, "section", -1)
    both, (w_gate, w_up, w_down) = gather_rows(
        jnp.concatenate([saved_input, incoming], axis=0), (w_gate, w_up, w_down)
    )
    inputs = both[0]
    upstream = both[1]
    f32 = jnp.float32
    gate = jnp.dot(inputs, w_gate, preferred_element_type=f32)
    up = jnp.dot(inputs, w_up, preferred_element_type=f32)
    sig = jax.nn.sigmoid(gate)
    act = gate * sig
    hidden = (act * up).astype(jnp.bfloat16)
    dhid = lax.dot_general(upstream, w_down, (((1,), (1,)), ((), ())), preferred_element_type=f32)
    grad_up_act = (dhid * act).astype(jnp.bfloat16)
    grad_gate_act = (dhid * up * sig * (1.0 + gate * (1.0 - sig))).astype(jnp.bfloat16)
    rows_t = (((0,), (0,)), ((), ()))
    tiles_gate = kept_in(lax.dot_general(inputs, grad_gate_act, rows_t, preferred_element_type=f32))
    tiles_up = kept_in(lax.dot_general(inputs, grad_up_act, rows_t, preferred_element_type=f32))
    tiles_down = kept_down(lax.dot_general(hidden, upstream, rows_t, preferred_element_type=f32))
    hid_t = (((1,), (1,)), ((), ()))
    whole_term = lax.dot_general(grad_gate_act, w_gate, hid_t, preferred_element_type=f32)
    whole_term = whole_term + lax.dot_general(
        grad_up_act, w_up, hid_t, preferred_element_type=f32
    )
    summed = scatter_rows(whole_term)
    grad_input = summed.astype(jnp.bfloat16)[None]
    return (grad_input, tiles_gate[None], tiles_up[None], tiles_down[None])


def solution(mesh):
    n_dp = mesh.shape["dp"]
    split = Mesh(
        mesh.devices.reshape(mesh.shape["section"], n_dp // 8, 4, 2),
        ("section",) + ROW_AXES,
    )
    rows = P("section", ROW_AXES, None)
    blocks = P("section", ROW_AXES, None, None)
    return jax.shard_map(
        per_device,
        mesh=split,
        in_specs=(rows, rows, P("section", ROW_AXES), blocks, blocks, blocks),
        out_specs=(rows, blocks, blocks, blocks),
        check_vma=False,
    )
```

```python
import jax
import jax.numpy as jnp
from jax import lax
from jax.sharding import Mesh, PartitionSpec as P

FF = 16384
ROW_AXES = ("y", "zh", "core")


def passed_along(block, axis, distance):
    devices = range(lax.axis_size(axis))
    route = [((i - distance) % len(devices), i) for i in devices]
    return lax.ppermute(block, axis, route)


def shifted(block, axis, shift):
    n = lax.axis_size(axis)
    return lax.ppermute(block, axis, [(i, (i + shift) % n) for i in range(n)])


def gather_rows(block, weights):
    n = lax.axis_size("zh")
    copies = jnp.broadcast_to(block[None], (n,) + block.shape)
    block = lax.all_to_all(copies, "zh", 0, 0, tiled=True)
    block = jnp.swapaxes(block, 0, 1).reshape(block.shape[1], -1, block.shape[3])
    block = lax.all_gather(block, "y", axis=1, tiled=True)
    block, weights = lax.optimization_barrier((block, weights))
    return (block, shifted(block, "core", 1)), weights


def scatter_rows(own, other):
    block = (own + shifted(other, "core", 1)).astype(jnp.bfloat16)
    block = lax.psum_scatter(block, "y", scatter_dimension=0, tiled=True)
    n = lax.axis_size("zh")
    chunks = block.reshape(n, -1, block.shape[1])
    got = lax.all_to_all(chunks, "zh", 0, 0, tiled=True)
    return jnp.sum(got.astype(jnp.float32), axis=0)


def per_device(saved_input, grad_sent, kept_blocks, gate_blocks, up_blocks, down_blocks):
    width = saved_input.shape[2]
    block = gate_blocks.shape[2]
    bands = width // block
    n_dp = 1
    for axis in ROW_AXES:
        n_dp *= lax.axis_size(axis)
    columns = FF // n_dp // block
    ids = kept_blocks[0]
    band_ids = ids // columns
    col_ids = ids % columns
    band_onehot = (band_ids[:, None] == jnp.arange(bands, dtype=jnp.int32)[None, :]).astype(
        jnp.bfloat16
    )
    col_onehot = (col_ids[:, None] == jnp.arange(columns, dtype=jnp.int32)[None, :]).astype(
        jnp.bfloat16
    )
    hidden_units = columns * block

    def dense_in(blocks):
        placed = jnp.einsum(
            "kr,kc,kbn->rbcn", band_onehot, col_onehot, blocks,
            preferred_element_type=jnp.float32,
        )
        return placed.astype(jnp.bfloat16).reshape(width, hidden_units)

    def dense_down(blocks):
        placed = jnp.einsum(
            "kc,kr,knb->cnrb", col_onehot, band_onehot, blocks,
            preferred_element_type=jnp.float32,
        )
        return placed.astype(jnp.bfloat16).reshape(hidden_units, width)

    def kept_in(dense):
        tiles = dense.astype(jnp.bfloat16).reshape(bands, block, columns, block)
        picked = jnp.einsum(
            "kr,kc,rbcn->kbn", band_onehot, col_onehot, tiles,
            preferred_element_type=jnp.float32,
        )
        return picked.astype(jnp.bfloat16)

    def kept_down(dense):
        tiles = dense.astype(jnp.bfloat16).reshape(columns, block, bands, block)
        picked = jnp.einsum(
            "kc,kr,cnrb->knb", col_onehot, band_onehot, tiles,
            preferred_element_type=jnp.float32,
        )
        return picked.astype(jnp.bfloat16)

    w_gate = dense_in(gate_blocks[0])
    w_up = dense_in(up_blocks[0])
    w_down = dense_down(down_blocks[0])

    incoming = passed_along(grad_sent, "section", -1)
    halves, (w_gate, w_up, w_down) = gather_rows(
        jnp.concatenate([saved_input, incoming], axis=0), (w_gate, w_up, w_down)
    )
    f32 = jnp.float32
    hid_t = (((1,), (1,)), ((), ()))

    def rows_part(both):
        inputs, upstream = both[0], both[1]
        gate = jnp.dot(inputs, w_gate, preferred_element_type=f32)
        up = jnp.dot(inputs, w_up, preferred_element_type=f32)
        sig = jax.nn.sigmoid(gate)
        act = gate * sig
        hidden = (act * up).astype(jnp.bfloat16)
        dhid = lax.dot_general(upstream, w_down, hid_t, preferred_element_type=f32)
        grad_up_act = (dhid * act).astype(jnp.bfloat16)
        grad_gate_act = (dhid * up * sig * (1.0 + gate * (1.0 - sig))).astype(jnp.bfloat16)
        term = lax.dot_general(grad_gate_act, w_gate, hid_t, preferred_element_type=f32)
        term = term + lax.dot_general(grad_up_act, w_up, hid_t, preferred_element_type=f32)
        return term, (inputs, upstream, hidden, grad_gate_act, grad_up_act)

    term_own, saved_own = rows_part(halves[0])
    term_other, saved_other = rows_part(halves[1])
    inputs, upstream, hidden, grad_gate_act, grad_up_act = (
        jnp.concatenate(pair, axis=0) for pair in zip(saved_own, saved_other)
    )
    rows_t = (((0,), (0,)), ((), ()))
    tiles_gate = kept_in(lax.dot_general(inputs, grad_gate_act, rows_t, preferred_element_type=f32))
    tiles_up = kept_in(lax.dot_general(inputs, grad_up_act, rows_t, preferred_element_type=f32))
    tiles_down = kept_down(lax.dot_general(hidden, upstream, rows_t, preferred_element_type=f32))
    summed = scatter_rows(term_own, term_other)
    grad_input = summed.astype(jnp.bfloat16)[None]
    return (grad_input, tiles_gate[None], tiles_up[None], tiles_down[None])


def solution(mesh):
    n_dp = mesh.shape["dp"]
    split = Mesh(
        mesh.devices.reshape(mesh.shape["section"], n_dp // 8, 4, 2),
        ("section",) + ROW_AXES,
    )
    rows = P("section", ROW_AXES, None)
    blocks = P("section", ROW_AXES, None, None)
    return jax.shard_map(
        per_device,
        mesh=split,
        in_specs=(rows, rows, P("section", ROW_AXES), blocks, blocks, blocks),
        out_specs=(rows, blocks, blocks, blocks),
        check_vma=False,
    )
```

```python
import jax
import jax.numpy as jnp
from jax import lax
from jax.sharding import Mesh, PartitionSpec as P

FF = 16384
ROW_AXES = ("y", "zh", "core")


def passed_along(block, axis, distance):
    devices = range(lax.axis_size(axis))
    route = [((i - distance) % len(devices), i) for i in devices]
    return lax.ppermute(block, axis, route)


def shifted(block, axis, shift):
    n = lax.axis_size(axis)
    return lax.ppermute(block, axis, [(i, (i + shift) % n) for i in range(n)])


def gather_rows(block, weights):
    n = lax.axis_size("zh")
    copies = jnp.tile(block, (n, 1))
    block = lax.all_to_all(copies, "zh", 0, 0, tiled=True)
    block = lax.all_gather(block, "y", axis=0, tiled=True)
    block, weights = lax.optimization_barrier((block, weights))
    return (block, shifted(block, "core", 1)), weights


def scatter_rows(own, other):
    block = (own + shifted(other, "core", 1)).astype(jnp.bfloat16)
    block = lax.psum_scatter(block, "y", scatter_dimension=0, tiled=True)
    n = lax.axis_size("zh")
    got = lax.all_to_all(block, "zh", 0, 0, tiled=True).astype(jnp.float32)
    own_rows = got.shape[0] // n
    total = got[:own_rows]
    for k in range(1, n):
        total = total + got[k * own_rows:(k + 1) * own_rows]
    return total


def per_device(saved_input, grad_sent, kept_blocks, gate_blocks, up_blocks, down_blocks):
    width = saved_input.shape[2]
    block = gate_blocks.shape[2]
    bands = width // block
    n_dp = 1
    for axis in ROW_AXES:
        n_dp *= lax.axis_size(axis)
    columns = FF // n_dp // block
    ids = kept_blocks[0]
    band_ids = ids // columns
    col_ids = ids % columns
    band_onehot = (band_ids[:, None] == jnp.arange(bands, dtype=jnp.int32)[None, :]).astype(
        jnp.bfloat16
    )
    col_onehot = (col_ids[:, None] == jnp.arange(columns, dtype=jnp.int32)[None, :]).astype(
        jnp.bfloat16
    )
    hidden_units = columns * block

    def dense_in(blocks):
        placed = jnp.einsum(
            "kr,kc,kbn->rbcn", band_onehot, col_onehot, blocks,
            preferred_element_type=jnp.float32,
        )
        return placed.astype(jnp.bfloat16).reshape(width, hidden_units)

    def dense_down(blocks):
        placed = jnp.einsum(
            "kc,kr,knb->cnrb", col_onehot, band_onehot, blocks,
            preferred_element_type=jnp.float32,
        )
        return placed.astype(jnp.bfloat16).reshape(hidden_units, width)

    def kept_in(dense):
        tiles = dense.astype(jnp.bfloat16).reshape(bands, block, columns, block)
        picked = jnp.einsum(
            "kr,kc,rbcn->kbn", band_onehot, col_onehot, tiles,
            preferred_element_type=jnp.float32,
        )
        return picked.astype(jnp.bfloat16)

    def kept_down(dense):
        tiles = dense.astype(jnp.bfloat16).reshape(columns, block, bands, block)
        picked = jnp.einsum(
            "kc,kr,cnrb->knb", col_onehot, band_onehot, tiles,
            preferred_element_type=jnp.float32,
        )
        return picked.astype(jnp.bfloat16)

    w_gate = dense_in(gate_blocks[0])
    w_up = dense_in(up_blocks[0])
    w_down = dense_down(down_blocks[0])

    incoming = passed_along(grad_sent, "section", -1)
    halves, (w_gate, w_up, w_down) = gather_rows(
        jnp.concatenate([saved_input[0], incoming[0]], axis=1), (w_gate, w_up, w_down)
    )
    f32 = jnp.float32
    hid_t = (((1,), (1,)), ((), ()))

    def rows_part(both):
        inputs, upstream = both[:, :width], both[:, width:]
        gate = jnp.dot(inputs, w_gate, preferred_element_type=f32)
        up = jnp.dot(inputs, w_up, preferred_element_type=f32)
        sig = jax.nn.sigmoid(gate)
        act = gate * sig
        hidden = (act * up).astype(jnp.bfloat16)
        dhid = lax.dot_general(upstream, w_down, hid_t, preferred_element_type=f32)
        grad_up_act = (dhid * act).astype(jnp.bfloat16)
        grad_gate_act = (dhid * up * sig * (1.0 + gate * (1.0 - sig))).astype(jnp.bfloat16)
        term = lax.dot_general(grad_gate_act, w_gate, hid_t, preferred_element_type=f32)
        term = term + lax.dot_general(grad_up_act, w_up, hid_t, preferred_element_type=f32)
        return term, (inputs, upstream, hidden, grad_gate_act, grad_up_act)

    term_own, saved_own = rows_part(halves[0])
    term_other, saved_other = rows_part(halves[1])
    inputs, upstream, hidden, grad_gate_act, grad_up_act = (
        jnp.concatenate(pair, axis=0) for pair in zip(saved_own, saved_other)
    )
    rows_t = (((0,), (0,)), ((), ()))
    tiles_gate = kept_in(lax.dot_general(inputs, grad_gate_act, rows_t, preferred_element_type=f32))
    tiles_up = kept_in(lax.dot_general(inputs, grad_up_act, rows_t, preferred_element_type=f32))
    tiles_down = kept_down(lax.dot_general(hidden, upstream, rows_t, preferred_element_type=f32))
    summed = scatter_rows(term_own, term_other)
    grad_input = summed.astype(jnp.bfloat16)[None]
    return (grad_input, tiles_gate[None], tiles_up[None], tiles_down[None])


def solution(mesh):
    n_dp = mesh.shape["dp"]
    split = Mesh(
        mesh.devices.reshape(mesh.shape["section"], n_dp // 8, 4, 2),
        ("section",) + ROW_AXES,
    )
    rows = P("section", ROW_AXES, None)
    blocks = P("section", ROW_AXES, None, None)
    return jax.shard_map(
        per_device,
        mesh=split,
        in_specs=(rows, rows, P("section", ROW_AXES), blocks, blocks, blocks),
        out_specs=(rows, blocks, blocks, blocks),
        check_vma=False,
    )
```

```python
import jax
import jax.numpy as jnp
from jax import lax
from jax.sharding import Mesh, PartitionSpec as P

FF = 16384
ROW_AXES = ("y", "zh", "core")


def passed_along(block, axis, distance):
    devices = range(lax.axis_size(axis))
    route = [((i - distance) % len(devices), i) for i in devices]
    return lax.ppermute(block, axis, route)


def shifted(block, axis, shift):
    n = lax.axis_size(axis)
    return lax.ppermute(block, axis, [(i, (i + shift) % n) for i in range(n)])


def gather_rows(block, weights):
    n = lax.axis_size("zh")
    copies = jnp.tile(block, (n, 1))
    block = lax.all_to_all(copies, "zh", 0, 0, tiled=True)
    block = lax.all_gather(block, "y", axis=0, tiled=True)
    block, weights = lax.optimization_barrier((block, weights))
    return (block, shifted(block, "core", 1)), weights


def scatter_rows(own, other):
    block = own + shifted(other, "core", 1)
    n_y, n_zh = lax.axis_size("y"), lax.axis_size("zh")
    by_zh = block.reshape(n_y, n_zh, -1, block.shape[1]).swapaxes(0, 1)
    by_zh = by_zh.reshape(-1, block.shape[1]).astype(jnp.bfloat16)
    got = lax.all_to_all(by_zh, "zh", 0, 0, tiled=True).astype(jnp.float32)
    part = got.shape[0] // n_zh
    total = got[:part]
    for k in range(1, n_zh):
        total = total + got[k * part:(k + 1) * part]
    total = lax.psum_scatter(total.astype(jnp.bfloat16), "y", scatter_dimension=0, tiled=True)
    return total.astype(jnp.float32)


def per_device(saved_input, grad_sent, kept_blocks, gate_blocks, up_blocks, down_blocks):
    width = saved_input.shape[2]
    block = gate_blocks.shape[2]
    bands = width // block
    n_dp = 1
    for axis in ROW_AXES:
        n_dp *= lax.axis_size(axis)
    columns = FF // n_dp // block
    ids = kept_blocks[0]
    band_ids = ids // columns
    col_ids = ids % columns
    band_onehot = (band_ids[:, None] == jnp.arange(bands, dtype=jnp.int32)[None, :]).astype(
        jnp.bfloat16
    )
    col_onehot = (col_ids[:, None] == jnp.arange(columns, dtype=jnp.int32)[None, :]).astype(
        jnp.bfloat16
    )
    hidden_units = columns * block

    def dense_in(blocks):
        placed = jnp.einsum(
            "kr,kc,kbn->rbcn", band_onehot, col_onehot, blocks,
            preferred_element_type=jnp.float32,
        )
        return placed.astype(jnp.bfloat16).reshape(width, hidden_units)

    def dense_down(blocks):
        placed = jnp.einsum(
            "kc,kr,knb->cnrb", col_onehot, band_onehot, blocks,
            preferred_element_type=jnp.float32,
        )
        return placed.astype(jnp.bfloat16).reshape(hidden_units, width)

    def kept_in(dense):
        tiles = dense.astype(jnp.bfloat16).reshape(bands, block, columns, block)
        picked = jnp.einsum(
            "kr,kc,rbcn->kbn", band_onehot, col_onehot, tiles,
            preferred_element_type=jnp.float32,
        )
        return picked.astype(jnp.bfloat16)

    def kept_down(dense):
        tiles = dense.astype(jnp.bfloat16).reshape(columns, block, bands, block)
        picked = jnp.einsum(
            "kc,kr,cnrb->knb", col_onehot, band_onehot, tiles,
            preferred_element_type=jnp.float32,
        )
        return picked.astype(jnp.bfloat16)

    w_gate = dense_in(gate_blocks[0])
    w_up = dense_in(up_blocks[0])
    w_down = dense_down(down_blocks[0])

    incoming = passed_along(grad_sent, "section", -1)
    halves, (w_gate, w_up, w_down) = gather_rows(
        jnp.concatenate([saved_input[0], incoming[0]], axis=1), (w_gate, w_up, w_down)
    )
    f32 = jnp.float32
    hid_t = (((1,), (1,)), ((), ()))

    def rows_part(both):
        inputs, upstream = both[:, :width], both[:, width:]
        gate = jnp.dot(inputs, w_gate, preferred_element_type=f32)
        up = jnp.dot(inputs, w_up, preferred_element_type=f32)
        sig = jax.nn.sigmoid(gate)
        act = gate * sig
        hidden = (act * up).astype(jnp.bfloat16)
        dhid = lax.dot_general(upstream, w_down, hid_t, preferred_element_type=f32)
        grad_up_act = (dhid * act).astype(jnp.bfloat16)
        grad_gate_act = (dhid * up * sig * (1.0 + gate * (1.0 - sig))).astype(jnp.bfloat16)
        term = lax.dot_general(grad_gate_act, w_gate, hid_t, preferred_element_type=f32)
        term = term + lax.dot_general(grad_up_act, w_up, hid_t, preferred_element_type=f32)
        return term, (inputs, upstream, hidden, grad_gate_act, grad_up_act)

    term_own, saved_own = rows_part(halves[0])
    term_other, saved_other = rows_part(halves[1])
    inputs, upstream, hidden, grad_gate_act, grad_up_act = (
        jnp.concatenate(pair, axis=0) for pair in zip(saved_own, saved_other)
    )
    rows_t = (((0,), (0,)), ((), ()))
    tiles_gate = kept_in(lax.dot_general(inputs, grad_gate_act, rows_t, preferred_element_type=f32))
    tiles_up = kept_in(lax.dot_general(inputs, grad_up_act, rows_t, preferred_element_type=f32))
    tiles_down = kept_down(lax.dot_general(hidden, upstream, rows_t, preferred_element_type=f32))
    summed = scatter_rows(term_own, term_other)
    grad_input = summed.astype(jnp.bfloat16)[None]
    return (grad_input, tiles_gate[None], tiles_up[None], tiles_down[None])


def solution(mesh):
    n_dp = mesh.shape["dp"]
    split = Mesh(
        mesh.devices.reshape(mesh.shape["section"], n_dp // 8, 4, 2),
        ("section",) + ROW_AXES,
    )
    rows = P("section", ROW_AXES, None)
    blocks = P("section", ROW_AXES, None, None)
    return jax.shard_map(
        per_device,
        mesh=split,
        in_specs=(rows, rows, P("section", ROW_AXES), blocks, blocks, blocks),
        out_specs=(rows, blocks, blocks, blocks),
        check_vma=False,
    )
```

```python
import jax
import jax.numpy as jnp
from jax import lax
from jax.sharding import Mesh, PartitionSpec as P

FF = 16384
ROW_AXES = ("y", "zh", "core")


def passed_along(block, axis, distance):
    devices = range(lax.axis_size(axis))
    route = [((i - distance) % len(devices), i) for i in devices]
    return lax.ppermute(block, axis, route)


def shifted(block, axis, shift):
    n = lax.axis_size(axis)
    return lax.ppermute(block, axis, [(i, (i + shift) % n) for i in range(n)])


def gather_rows(block, weights):
    block = jnp.concatenate([block, shifted(block, "core", 1)], axis=0)
    n = lax.axis_size("zh")
    copies = jnp.tile(block, (n, 1))
    block = lax.all_to_all(copies, "zh", 0, 0, tiled=True)
    block = lax.all_gather(block, "y", axis=0, tiled=True)
    block, weights = lax.optimization_barrier((block, weights))
    pairs = block.reshape(-1, 2, block.shape[0] // (2 * lax.axis_size("y") * n), block.shape[1])
    return (
        pairs[:, 0].reshape(-1, block.shape[1]),
        pairs[:, 1].reshape(-1, block.shape[1]),
    ), weights


def scatter_rows(own, other):
    block = (own + shifted(other, "core", 1)).astype(jnp.bfloat16)
    block = lax.psum_scatter(block, "y", scatter_dimension=0, tiled=True)
    n = lax.axis_size("zh")
    got = lax.all_to_all(block, "zh", 0, 0, tiled=True).astype(jnp.float32)
    own_rows = got.shape[0] // n
    total = got[:own_rows]
    for k in range(1, n):
        total = total + got[k * own_rows:(k + 1) * own_rows]
    return total


def per_device(saved_input, grad_sent, kept_blocks, gate_blocks, up_blocks, down_blocks):
    width = saved_input.shape[2]
    block = gate_blocks.shape[2]
    bands = width // block
    n_dp = 1
    for axis in ROW_AXES:
        n_dp *= lax.axis_size(axis)
    columns = FF // n_dp // block
    ids = kept_blocks[0]
    band_ids = ids // columns
    col_ids = ids % columns
    band_onehot = (band_ids[:, None] == jnp.arange(bands, dtype=jnp.int32)[None, :]).astype(
        jnp.bfloat16
    )
    col_onehot = (col_ids[:, None] == jnp.arange(columns, dtype=jnp.int32)[None, :]).astype(
        jnp.bfloat16
    )
    hidden_units = columns * block

    def dense_in(blocks):
        placed = jnp.einsum(
            "kr,kc,kbn->rbcn", band_onehot, col_onehot, blocks,
            preferred_element_type=jnp.float32,
        )
        return placed.astype(jnp.bfloat16).reshape(width, hidden_units)

    def dense_down(blocks):
        placed = jnp.einsum(
            "kc,kr,knb->cnrb", col_onehot, band_onehot, blocks,
            preferred_element_type=jnp.float32,
        )
        return placed.astype(jnp.bfloat16).reshape(hidden_units, width)

    def kept_in(dense):
        tiles = dense.astype(jnp.bfloat16).reshape(bands, block, columns, block)
        picked = jnp.einsum(
            "kr,kc,rbcn->kbn", band_onehot, col_onehot, tiles,
            preferred_element_type=jnp.float32,
        )
        return picked.astype(jnp.bfloat16)

    def kept_down(dense):
        tiles = dense.astype(jnp.bfloat16).reshape(columns, block, bands, block)
        picked = jnp.einsum(
            "kc,kr,cnrb->knb", col_onehot, band_onehot, tiles,
            preferred_element_type=jnp.float32,
        )
        return picked.astype(jnp.bfloat16)

    w_gate = dense_in(gate_blocks[0])
    w_up = dense_in(up_blocks[0])
    w_down = dense_down(down_blocks[0])

    incoming = passed_along(grad_sent, "section", -1)
    halves, (w_gate, w_up, w_down) = gather_rows(
        jnp.concatenate([saved_input[0], incoming[0]], axis=1), (w_gate, w_up, w_down)
    )
    f32 = jnp.float32
    hid_t = (((1,), (1,)), ((), ()))

    def rows_part(both):
        inputs, upstream = both[:, :width], both[:, width:]
        gate = jnp.dot(inputs, w_gate, preferred_element_type=f32)
        up = jnp.dot(inputs, w_up, preferred_element_type=f32)
        sig = jax.nn.sigmoid(gate)
        act = gate * sig
        hidden = (act * up).astype(jnp.bfloat16)
        dhid = lax.dot_general(upstream, w_down, hid_t, preferred_element_type=f32)
        grad_up_act = (dhid * act).astype(jnp.bfloat16)
        grad_gate_act = (dhid * up * sig * (1.0 + gate * (1.0 - sig))).astype(jnp.bfloat16)
        term = lax.dot_general(grad_gate_act, w_gate, hid_t, preferred_element_type=f32)
        term = term + lax.dot_general(grad_up_act, w_up, hid_t, preferred_element_type=f32)
        return term, (inputs, upstream, hidden, grad_gate_act, grad_up_act)

    term_own, saved_own = rows_part(halves[0])
    term_other, saved_other = rows_part(halves[1])
    inputs, upstream, hidden, grad_gate_act, grad_up_act = (
        jnp.concatenate(pair, axis=0) for pair in zip(saved_own, saved_other)
    )
    rows_t = (((0,), (0,)), ((), ()))
    tiles_gate = kept_in(lax.dot_general(inputs, grad_gate_act, rows_t, preferred_element_type=f32))
    tiles_up = kept_in(lax.dot_general(inputs, grad_up_act, rows_t, preferred_element_type=f32))
    tiles_down = kept_down(lax.dot_general(hidden, upstream, rows_t, preferred_element_type=f32))
    summed = scatter_rows(term_own, term_other)
    grad_input = summed.astype(jnp.bfloat16)[None]
    return (grad_input, tiles_gate[None], tiles_up[None], tiles_down[None])


def solution(mesh):
    n_dp = mesh.shape["dp"]
    split = Mesh(
        mesh.devices.reshape(mesh.shape["section"], n_dp // 8, 4, 2),
        ("section",) + ROW_AXES,
    )
    rows = P("section", ROW_AXES, None)
    blocks = P("section", ROW_AXES, None, None)
    return jax.shard_map(
        per_device,
        mesh=split,
        in_specs=(rows, rows, P("section", ROW_AXES), blocks, blocks, blocks),
        out_specs=(rows, blocks, blocks, blocks),
        check_vma=False,
    )
```

```python
import jax
import jax.numpy as jnp
from jax import lax
from jax.sharding import Mesh, PartitionSpec as P

FF = 16384
ROW_AXES = ("y", "zh", "core")


def passed_along(block, axis, distance):
    devices = range(lax.axis_size(axis))
    route = [((i - distance) % len(devices), i) for i in devices]
    return lax.ppermute(block, axis, route)


def shifted(block, axis, shift):
    n = lax.axis_size(axis)
    return lax.ppermute(block, axis, [(i, (i + shift) % n) for i in range(n)])


def gather_rows(block, weights):
    n = lax.axis_size("zh")
    copies = jnp.tile(block, (n, 1))
    block = lax.all_to_all(copies, "zh", 0, 0, tiled=True)
    block = lax.all_gather(block, "y", axis=0, tiled=True)
    block, weights = lax.optimization_barrier((block, weights))
    return (block, shifted(block, "core", 1)), weights


def scatter_rows(block):
    block = block.astype(jnp.bfloat16)
    block = lax.psum_scatter(block, "y", scatter_dimension=0, tiled=True)
    n = lax.axis_size("zh")
    got = lax.all_to_all(block, "zh", 0, 0, tiled=True).astype(jnp.float32)
    own_rows = got.shape[0] // n
    total = got[:own_rows]
    for k in range(1, n):
        total = total + got[k * own_rows:(k + 1) * own_rows]
    return total


def per_device(saved_input, grad_sent, kept_blocks, gate_blocks, up_blocks, down_blocks):
    width = saved_input.shape[2]
    block = gate_blocks.shape[2]
    bands = width // block
    n_dp = 1
    for axis in ROW_AXES:
        n_dp *= lax.axis_size(axis)
    columns = FF // n_dp // block
    ids = kept_blocks[0]
    band_ids = ids // columns
    col_ids = ids % columns
    band_onehot = (band_ids[:, None] == jnp.arange(bands, dtype=jnp.int32)[None, :]).astype(
        jnp.bfloat16
    )
    col_onehot = (col_ids[:, None] == jnp.arange(columns, dtype=jnp.int32)[None, :]).astype(
        jnp.bfloat16
    )
    hidden_units = columns * block

    def dense_in(blocks):
        placed = jnp.einsum(
            "kr,kc,kbn->rbcn", band_onehot, col_onehot, blocks,
            preferred_element_type=jnp.float32,
        )
        return placed.astype(jnp.bfloat16).reshape(width, hidden_units)

    def dense_down(blocks):
        placed = jnp.einsum(
            "kc,kr,knb->cnrb", col_onehot, band_onehot, blocks,
            preferred_element_type=jnp.float32,
        )
        return placed.astype(jnp.bfloat16).reshape(hidden_units, width)

    def kept_in(dense):
        tiles = dense.astype(jnp.bfloat16).reshape(bands, block, columns, block)
        picked = jnp.einsum(
            "kr,kc,rbcn->kbn", band_onehot, col_onehot, tiles,
            preferred_element_type=jnp.float32,
        )
        return picked.astype(jnp.bfloat16)

    def kept_down(dense):
        tiles = dense.astype(jnp.bfloat16).reshape(columns, block, bands, block)
        picked = jnp.einsum(
            "kc,kr,cnrb->knb", col_onehot, band_onehot, tiles,
            preferred_element_type=jnp.float32,
        )
        return picked.astype(jnp.bfloat16)

    w_gate = dense_in(gate_blocks[0])
    w_up = dense_in(up_blocks[0])
    w_down = dense_down(down_blocks[0])

    incoming = passed_along(grad_sent, "section", -1)
    w_gate = jnp.concatenate([w_gate, shifted(w_gate, "core", 1)], axis=1)
    w_up = jnp.concatenate([w_up, shifted(w_up, "core", 1)], axis=1)
    w_down = jnp.concatenate([w_down, shifted(w_down, "core", 1)], axis=0)
    (both, other_rows), (w_gate, w_up, w_down) = gather_rows(
        jnp.concatenate([saved_input[0], incoming[0]], axis=1), (w_gate, w_up, w_down)
    )
    f32 = jnp.float32
    hid_t = (((1,), (1,)), ((), ()))
    inputs, upstream = both[:, :width], both[:, width:]
    gate = jnp.dot(inputs, w_gate, preferred_element_type=f32)
    up = jnp.dot(inputs, w_up, preferred_element_type=f32)
    sig = jax.nn.sigmoid(gate)
    act = gate * sig
    hidden = (act * up).astype(jnp.bfloat16)
    dhid = lax.dot_general(upstream, w_down, hid_t, preferred_element_type=f32)
    grad_up_act = (dhid * act).astype(jnp.bfloat16)
    grad_gate_act = (dhid * up * sig * (1.0 + gate * (1.0 - sig))).astype(jnp.bfloat16)
    whole_term = lax.dot_general(grad_gate_act, w_gate, hid_t, preferred_element_type=f32)
    whole_term = whole_term + lax.dot_general(
        grad_up_act, w_up, hid_t, preferred_element_type=f32
    )
    summed = scatter_rows(whole_term)

    def own_and_partner(values):
        sent = shifted(values[:, hidden_units:], "core", 1)
        return jnp.concatenate([values[:, :hidden_units], sent], axis=0)

    grad_gate_act, grad_up_act, hidden = (
        own_and_partner(v) for v in (grad_gate_act, grad_up_act, hidden)
    )
    inputs = jnp.concatenate([inputs, other_rows[:, :width]], axis=0)
    upstream = jnp.concatenate([upstream, other_rows[:, width:]], axis=0)
    rows_t = (((0,), (0,)), ((), ()))
    tiles_gate = kept_in(lax.dot_general(inputs, grad_gate_act, rows_t, preferred_element_type=f32))
    tiles_up = kept_in(lax.dot_general(inputs, grad_up_act, rows_t, preferred_element_type=f32))
    tiles_down = kept_down(lax.dot_general(hidden, upstream, rows_t, preferred_element_type=f32))
    grad_input = summed.astype(jnp.bfloat16)[None]
    return (grad_input, tiles_gate[None], tiles_up[None], tiles_down[None])


def solution(mesh):
    n_dp = mesh.shape["dp"]
    split = Mesh(
        mesh.devices.reshape(mesh.shape["section"], n_dp // 8, 4, 2),
        ("section",) + ROW_AXES,
    )
    rows = P("section", ROW_AXES, None)
    blocks = P("section", ROW_AXES, None, None)
    return jax.shard_map(
        per_device,
        mesh=split,
        in_specs=(rows, rows, P("section", ROW_AXES), blocks, blocks, blocks),
        out_specs=(rows, blocks, blocks, blocks),
        check_vma=False,
    )
```

```python
import jax
import jax.numpy as jnp
from jax import lax
from jax.sharding import Mesh, PartitionSpec as P

FF = 16384
ROW_AXES = ("y", "zh", "core")


def passed_along(block, axis, distance):
    devices = range(lax.axis_size(axis))
    route = [((i - distance) % len(devices), i) for i in devices]
    return lax.ppermute(block, axis, route)


def shifted(block, axis, shift):
    n = lax.axis_size(axis)
    return lax.ppermute(block, axis, [(i, (i + shift) % n) for i in range(n)])


def gather_rows(block, weights):
    n = lax.axis_size("zh")
    copies = jnp.tile(block, (n, 1))
    block = lax.all_to_all(copies, "zh", 0, 0, tiled=True)
    block = lax.all_gather(block, "y", axis=0, tiled=True)
    block, weights = lax.optimization_barrier((block, weights))
    return (block, shifted(block, "core", 1)), weights


def scatter_rows(block):
    block = block.astype(jnp.bfloat16)
    block = lax.psum_scatter(block, "y", scatter_dimension=0, tiled=True)
    n = lax.axis_size("zh")
    got = lax.all_to_all(block, "zh", 0, 0, tiled=True).astype(jnp.float32)
    own_rows = got.shape[0] // n
    total = got[:own_rows]
    for k in range(1, n):
        total = total + got[k * own_rows:(k + 1) * own_rows]
    return total


def per_device(saved_input, grad_sent, kept_blocks, gate_blocks, up_blocks, down_blocks):
    width = saved_input.shape[2]
    block = gate_blocks.shape[2]
    bands = width // block
    n_dp = 1
    for axis in ROW_AXES:
        n_dp *= lax.axis_size(axis)
    columns = FF // n_dp // block
    ids = kept_blocks[0]
    band_ids = ids // columns
    col_ids = ids % columns
    band_onehot = (band_ids[:, None] == jnp.arange(bands, dtype=jnp.int32)[None, :]).astype(
        jnp.bfloat16
    )
    col_onehot = (col_ids[:, None] == jnp.arange(columns, dtype=jnp.int32)[None, :]).astype(
        jnp.bfloat16
    )
    hidden_units = columns * block

    def dense_in(blocks):
        placed = jnp.einsum(
            "kr,kc,kbn->rbcn", band_onehot, col_onehot, blocks,
            preferred_element_type=jnp.float32,
        )
        return placed.astype(jnp.bfloat16).reshape(width, hidden_units)

    def dense_down(blocks):
        placed = jnp.einsum(
            "kc,kr,knb->cnrb", col_onehot, band_onehot, blocks,
            preferred_element_type=jnp.float32,
        )
        return placed.astype(jnp.bfloat16).reshape(hidden_units, width)

    def kept_in(dense):
        tiles = dense.astype(jnp.bfloat16).reshape(bands, block, columns, block)
        picked = jnp.einsum(
            "kr,kc,rbcn->kbn", band_onehot, col_onehot, tiles,
            preferred_element_type=jnp.float32,
        )
        return picked.astype(jnp.bfloat16)

    def kept_down(dense):
        tiles = dense.astype(jnp.bfloat16).reshape(columns, block, bands, block)
        picked = jnp.einsum(
            "kc,kr,cnrb->knb", col_onehot, band_onehot, tiles,
            preferred_element_type=jnp.float32,
        )
        return picked.astype(jnp.bfloat16)

    w_gate = dense_in(gate_blocks[0])
    w_up = dense_in(up_blocks[0])
    w_down = dense_down(down_blocks[0])

    incoming = passed_along(grad_sent, "section", -1)
    weights = (w_gate, w_up, w_down)
    partner_weights = tuple(shifted(w, "core", 1) for w in weights)
    (both, other_rows), (weights, partner_weights) = gather_rows(
        jnp.concatenate([saved_input[0], incoming[0]], axis=1), (weights, partner_weights)
    )
    f32 = jnp.float32
    hid_t = (((1,), (1,)), ((), ()))
    inputs, upstream = both[:, :width], both[:, width:]

    def units_part(wg, wu, wd):
        gate = jnp.dot(inputs, wg, preferred_element_type=f32)
        up = jnp.dot(inputs, wu, preferred_element_type=f32)
        sig = jax.nn.sigmoid(gate)
        act = gate * sig
        hidden = (act * up).astype(jnp.bfloat16)
        dhid = lax.dot_general(upstream, wd, hid_t, preferred_element_type=f32)
        grad_up_act = (dhid * act).astype(jnp.bfloat16)
        grad_gate_act = (dhid * up * sig * (1.0 + gate * (1.0 - sig))).astype(jnp.bfloat16)
        term = lax.dot_general(grad_gate_act, wg, hid_t, preferred_element_type=f32)
        term = term + lax.dot_general(grad_up_act, wu, hid_t, preferred_element_type=f32)
        return term, (grad_gate_act, grad_up_act, hidden)

    term_own, acts_own = units_part(*weights)
    term_partner, acts_partner = units_part(*partner_weights)
    summed = scatter_rows(term_own + term_partner)

    grad_gate_act, grad_up_act, hidden = (
        jnp.concatenate([mine, shifted(theirs, "core", 1)], axis=0)
        for mine, theirs in zip(acts_own, acts_partner)
    )
    inputs = jnp.concatenate([inputs, other_rows[:, :width]], axis=0)
    upstream = jnp.concatenate([upstream, other_rows[:, width:]], axis=0)
    rows_t = (((0,), (0,)), ((), ()))
    tiles_gate = kept_in(lax.dot_general(inputs, grad_gate_act, rows_t, preferred_element_type=f32))
    tiles_up = kept_in(lax.dot_general(inputs, grad_up_act, rows_t, preferred_element_type=f32))
    tiles_down = kept_down(lax.dot_general(hidden, upstream, rows_t, preferred_element_type=f32))
    grad_input = summed.astype(jnp.bfloat16)[None]
    return (grad_input, tiles_gate[None], tiles_up[None], tiles_down[None])


def solution(mesh):
    n_dp = mesh.shape["dp"]
    split = Mesh(
        mesh.devices.reshape(mesh.shape["section"], n_dp // 8, 4, 2),
        ("section",) + ROW_AXES,
    )
    rows = P("section", ROW_AXES, None)
    blocks = P("section", ROW_AXES, None, None)
    return jax.shard_map(
        per_device,
        mesh=split,
        in_specs=(rows, rows, P("section", ROW_AXES), blocks, blocks, blocks),
        out_specs=(rows, blocks, blocks, blocks),
        check_vma=False,
    )
```

```python
import jax
import jax.numpy as jnp
from jax import lax
from jax.sharding import Mesh, PartitionSpec as P

FF = 16384
ROW_AXES = ("y", "zh", "core")


def passed_along(block, axis, distance):
    devices = range(lax.axis_size(axis))
    route = [((i - distance) % len(devices), i) for i in devices]
    return lax.ppermute(block, axis, route)


def shifted(block, axis, shift):
    n = lax.axis_size(axis)
    return lax.ppermute(block, axis, [(i, (i + shift) % n) for i in range(n)])


def gather_rows(block, weights):
    block = lax.all_gather(block, "zh", axis=0, tiled=True)
    block = lax.all_gather(block, "y", axis=0, tiled=True)
    block, weights = lax.optimization_barrier((block, weights))
    return (block, shifted(block, "core", 1)), weights


def scatter_rows(own, other):
    block = (own + shifted(other, "core", 1)).astype(jnp.bfloat16)
    block = lax.psum_scatter(block, "y", scatter_dimension=0, tiled=True)
    n = lax.axis_size("zh")
    got = lax.all_to_all(block, "zh", 0, 0, tiled=True).astype(jnp.float32)
    own_rows = got.shape[0] // n
    total = got[:own_rows]
    for k in range(1, n):
        total = total + got[k * own_rows:(k + 1) * own_rows]
    return total


def per_device(saved_input, grad_sent, kept_blocks, gate_blocks, up_blocks, down_blocks):
    width = saved_input.shape[2]
    block = gate_blocks.shape[2]
    bands = width // block
    n_dp = 1
    for axis in ROW_AXES:
        n_dp *= lax.axis_size(axis)
    columns = FF // n_dp // block
    ids = kept_blocks[0]
    band_ids = ids // columns
    col_ids = ids % columns
    band_onehot = (band_ids[:, None] == jnp.arange(bands, dtype=jnp.int32)[None, :]).astype(
        jnp.bfloat16
    )
    col_onehot = (col_ids[:, None] == jnp.arange(columns, dtype=jnp.int32)[None, :]).astype(
        jnp.bfloat16
    )
    hidden_units = columns * block

    def dense_in(blocks):
        placed = jnp.einsum(
            "kr,kc,kbn->rbcn", band_onehot, col_onehot, blocks,
            preferred_element_type=jnp.float32,
        )
        return placed.astype(jnp.bfloat16).reshape(width, hidden_units)

    def dense_down(blocks):
        placed = jnp.einsum(
            "kc,kr,knb->cnrb", col_onehot, band_onehot, blocks,
            preferred_element_type=jnp.float32,
        )
        return placed.astype(jnp.bfloat16).reshape(hidden_units, width)

    def kept_in(dense):
        tiles = dense.astype(jnp.bfloat16).reshape(bands, block, columns, block)
        picked = jnp.einsum(
            "kr,kc,rbcn->kbn", band_onehot, col_onehot, tiles,
            preferred_element_type=jnp.float32,
        )
        return picked.astype(jnp.bfloat16)

    def kept_down(dense):
        tiles = dense.astype(jnp.bfloat16).reshape(columns, block, bands, block)
        picked = jnp.einsum(
            "kc,kr,cnrb->knb", col_onehot, band_onehot, tiles,
            preferred_element_type=jnp.float32,
        )
        return picked.astype(jnp.bfloat16)

    w_gate = dense_in(gate_blocks[0])
    w_up = dense_in(up_blocks[0])
    w_down = dense_down(down_blocks[0])

    incoming = passed_along(grad_sent, "section", -1)
    halves, (w_gate, w_up, w_down) = gather_rows(
        jnp.concatenate([saved_input[0], incoming[0]], axis=1), (w_gate, w_up, w_down)
    )
    f32 = jnp.float32
    hid_t = (((1,), (1,)), ((), ()))

    def rows_part(both):
        inputs, upstream = both[:, :width], both[:, width:]
        gate = jnp.dot(inputs, w_gate, preferred_element_type=f32)
        up = jnp.dot(inputs, w_up, preferred_element_type=f32)
        sig = jax.nn.sigmoid(gate)
        act = gate * sig
        hidden = (act * up).astype(jnp.bfloat16)
        dhid = lax.dot_general(upstream, w_down, hid_t, preferred_element_type=f32)
        grad_up_act = (dhid * act).astype(jnp.bfloat16)
        grad_gate_act = (dhid * up * sig * (1.0 + gate * (1.0 - sig))).astype(jnp.bfloat16)
        term = lax.dot_general(grad_gate_act, w_gate, hid_t, preferred_element_type=f32)
        term = term + lax.dot_general(grad_up_act, w_up, hid_t, preferred_element_type=f32)
        return term, (inputs, upstream, hidden, grad_gate_act, grad_up_act)

    term_own, saved_own = rows_part(halves[0])
    term_other, saved_other = rows_part(halves[1])
    inputs, upstream, hidden, grad_gate_act, grad_up_act = (
        jnp.concatenate(pair, axis=0) for pair in zip(saved_own, saved_other)
    )
    rows_t = (((0,), (0,)), ((), ()))
    tiles_gate = kept_in(lax.dot_general(inputs, grad_gate_act, rows_t, preferred_element_type=f32))
    tiles_up = kept_in(lax.dot_general(inputs, grad_up_act, rows_t, preferred_element_type=f32))
    tiles_down = kept_down(lax.dot_general(hidden, upstream, rows_t, preferred_element_type=f32))
    summed = scatter_rows(term_own, term_other)
    grad_input = summed.astype(jnp.bfloat16)[None]
    return (grad_input, tiles_gate[None], tiles_up[None], tiles_down[None])


def solution(mesh):
    n_dp = mesh.shape["dp"]
    split = Mesh(
        mesh.devices.reshape(mesh.shape["section"], n_dp // 8, 4, 2),
        ("section",) + ROW_AXES,
    )
    rows = P("section", ROW_AXES, None)
    blocks = P("section", ROW_AXES, None, None)
    return jax.shard_map(
        per_device,
        mesh=split,
        in_specs=(rows, rows, P("section", ROW_AXES), blocks, blocks, blocks),
        out_specs=(rows, blocks, blocks, blocks),
        check_vma=False,
    )
```

```python
import jax
import jax.numpy as jnp
from jax import lax
from jax.sharding import Mesh, PartitionSpec as P

FF = 16384
ROW_AXES = ("y", "zh", "core")


def passed_along(block, axis, distance):
    devices = range(lax.axis_size(axis))
    route = [((i - distance) % len(devices), i) for i in devices]
    return lax.ppermute(block, axis, route)


def shifted(block, axis, shift):
    n = lax.axis_size(axis)
    return lax.ppermute(block, axis, [(i, (i + shift) % n) for i in range(n)])


def gather_rows(block, weights):
    n = lax.axis_size("zh")
    copies = jnp.tile(block, (n, 1))
    block = lax.all_to_all(copies, "zh", 0, 0, tiled=True)
    block = lax.all_gather(block, "y", axis=0, tiled=True)
    block, weights = lax.optimization_barrier((block, weights))
    return (block, shifted(block, "core", 1)), weights


def scatter_rows(own, other):
    sent = shifted(other.astype(jnp.bfloat16), "core", 1)
    block = (own + sent.astype(jnp.float32)).astype(jnp.bfloat16)
    block = lax.psum_scatter(block, "y", scatter_dimension=0, tiled=True)
    n = lax.axis_size("zh")
    got = lax.all_to_all(block, "zh", 0, 0, tiled=True).astype(jnp.float32)
    own_rows = got.shape[0] // n
    total = got[:own_rows]
    for k in range(1, n):
        total = total + got[k * own_rows:(k + 1) * own_rows]
    return total


def per_device(saved_input, grad_sent, kept_blocks, gate_blocks, up_blocks, down_blocks):
    width = saved_input.shape[2]
    block = gate_blocks.shape[2]
    bands = width // block
    n_dp = 1
    for axis in ROW_AXES:
        n_dp *= lax.axis_size(axis)
    columns = FF // n_dp // block
    ids = kept_blocks[0]
    band_ids = ids // columns
    col_ids = ids % columns
    band_onehot = (band_ids[:, None] == jnp.arange(bands, dtype=jnp.int32)[None, :]).astype(
        jnp.bfloat16
    )
    col_onehot = (col_ids[:, None] == jnp.arange(columns, dtype=jnp.int32)[None, :]).astype(
        jnp.bfloat16
    )
    hidden_units = columns * block

    def dense_in(blocks):
        placed = jnp.einsum(
            "kr,kc,kbn->rbcn", band_onehot, col_onehot, blocks,
            preferred_element_type=jnp.float32,
        )
        return placed.astype(jnp.bfloat16).reshape(width, hidden_units)

    def dense_down(blocks):
        placed = jnp.einsum(
            "kc,kr,knb->cnrb", col_onehot, band_onehot, blocks,
            preferred_element_type=jnp.float32,
        )
        return placed.astype(jnp.bfloat16).reshape(hidden_units, width)

    def kept_in(dense):
        tiles = dense.astype(jnp.bfloat16).reshape(bands, block, columns, block)
        picked = jnp.einsum(
            "kr,kc,rbcn->kbn", band_onehot, col_onehot, tiles,
            preferred_element_type=jnp.float32,
        )
        return picked.astype(jnp.bfloat16)

    def kept_down(dense):
        tiles = dense.astype(jnp.bfloat16).reshape(columns, block, bands, block)
        picked = jnp.einsum(
            "kc,kr,cnrb->knb", col_onehot, band_onehot, tiles,
            preferred_element_type=jnp.float32,
        )
        return picked.astype(jnp.bfloat16)

    w_gate = dense_in(gate_blocks[0])
    w_up = dense_in(up_blocks[0])
    w_down = dense_down(down_blocks[0])

    incoming = passed_along(grad_sent, "section", -1)
    halves, (w_gate, w_up, w_down) = gather_rows(
        jnp.concatenate([saved_input[0], incoming[0]], axis=1), (w_gate, w_up, w_down)
    )
    f32 = jnp.float32
    hid_t = (((1,), (1,)), ((), ()))

    def rows_part(both):
        inputs, upstream = both[:, :width], both[:, width:]
        gate = jnp.dot(inputs, w_gate, preferred_element_type=f32)
        up = jnp.dot(inputs, w_up, preferred_element_type=f32)
        sig = jax.nn.sigmoid(gate)
        act = gate * sig
        hidden = (act * up).astype(jnp.bfloat16)
        dhid = lax.dot_general(upstream, w_down, hid_t, preferred_element_type=f32)
        grad_up_act = (dhid * act).astype(jnp.bfloat16)
        grad_gate_act = (dhid * up * sig * (1.0 + gate * (1.0 - sig))).astype(jnp.bfloat16)
        term = lax.dot_general(grad_gate_act, w_gate, hid_t, preferred_element_type=f32)
        term = term + lax.dot_general(grad_up_act, w_up, hid_t, preferred_element_type=f32)
        return term, (inputs, upstream, hidden, grad_gate_act, grad_up_act)

    term_own, saved_own = rows_part(halves[0])
    term_other, saved_other = rows_part(halves[1])
    inputs, upstream, hidden, grad_gate_act, grad_up_act = (
        jnp.concatenate(pair, axis=0) for pair in zip(saved_own, saved_other)
    )
    rows_t = (((0,), (0,)), ((), ()))
    tiles_gate = kept_in(lax.dot_general(inputs, grad_gate_act, rows_t, preferred_element_type=f32))
    tiles_up = kept_in(lax.dot_general(inputs, grad_up_act, rows_t, preferred_element_type=f32))
    tiles_down = kept_down(lax.dot_general(hidden, upstream, rows_t, preferred_element_type=f32))
    summed = scatter_rows(term_own, term_other)
    grad_input = summed.astype(jnp.bfloat16)[None]
    return (grad_input, tiles_gate[None], tiles_up[None], tiles_down[None])


def solution(mesh):
    n_dp = mesh.shape["dp"]
    split = Mesh(
        mesh.devices.reshape(mesh.shape["section"], n_dp // 8, 4, 2),
        ("section",) + ROW_AXES,
    )
    rows = P("section", ROW_AXES, None)
    blocks = P("section", ROW_AXES, None, None)
    return jax.shard_map(
        per_device,
        mesh=split,
        in_specs=(rows, rows, P("section", ROW_AXES), blocks, blocks, blocks),
        out_specs=(rows, blocks, blocks, blocks),
        check_vma=False,
    )
```
